32 devices in a mesh: pb: 8 (over z, y), col: 4 (over x, core).
Axes of the slice: x: 2, y: 2, z: 4, core: 2. Of those that a mesh axis runs over, the one named last changes fastest.
Arguments:
- orbitals: bfloat16 [8, 48, 4096], P('pb', None, 'col'), may hold values from -6 to 6
- screening: bfloat16 [8, 4096, 4096], P('pb', None, 'col'), may hold values from -0.0014648438 to 0.0014648438
- pairs_k: int32 [8, 4], P('pb'), may hold values from 0 to 7
Outputs:
- kernel: float32 [8, 4, 256, 1024], P('pb', None, None, 'col')
The draws below stay inside these ranges and needn't reach their ends.
All inputs are finite; a program needn't handle non-finite values.
Results may differ from the reference program's by a relative error of at most 0.0049.
Values may be sent and summed in bfloat16 or wider, within the bound.
No kernel may reach another device: no remote copies, remote signals or barrier semaphores. Data moves between devices by JAX's collectives and lax.ppermute only.
A program may use at most 128 MiB of HBM per device.

```python
import jax
import jax.numpy as jnp
from jax import lax

NV = 16
NC = 32
NMU = 4096
PAIRS = 4
NK = 8
NQ = 8


def with_ends(array, stream_key, least, top_value):
    longest = array.shape.index(max(array.shape))
    spots = []
    for shift in (0, 1):
        where = [jax.random.randint(jax.random.fold_in(stream_key, axis), (), 0, length) for axis, length in enumerate(array.shape)]
        where[longest] = (where[longest] + shift) % array.shape[longest]
        spots.append(tuple(where))
    return array.at[spots[0]].set(least).at[spots[1]].set(top_value)


def block_levels(own_key, shape, split, smallest, top_value):
    level = 1.0
    for axis_at, shards_of in split:
        heights = jax.random.uniform(jax.random.fold_in(jax.random.fold_in(own_key, 6), axis_at), (shards_of,), jnp.float32, smallest / len(split), top_value / len(split))
        level = level * jnp.repeat(jnp.exp(heights), shape[axis_at] // shards_of).reshape((-1,) + (1,) * (len(shape) - 1 - axis_at))
    return level


def normal_values(own_key, shape, spread, limit, cuts=(), held_as=jnp.bfloat16):
    loudness = block_levels(own_key, shape, cuts, -0.22, 0.18) if cuts else 1.0
    result = jax.random.normal(own_key, shape, jnp.float32) * spread * loudness
    return jnp.minimum(jnp.maximum(result, -limit), limit).astype(held_as)


def setup_inputs(seed: int = 0) -> dict:
    keys = jax.random.split(jax.random.key(seed), 4)
    return {
        "orbitals": normal_values(keys[0], (NK, NV + NC, NMU), 1.0, 6.0, ((0, 8), (2, 4))),
        "screening": normal_values(keys[1], (NQ, NMU, NMU), (1.0 / NMU), 0.0014648438, ((0, 8), (2, 4))),
        "pairs_k": with_ends(jax.random.randint(keys[2], (NQ, PAIRS), 0, NK), jax.random.fold_in(keys[2], 1), 0, NK - 1).astype(jnp.int32),
    }


def reference(orbitals, screening, pairs_k):
    kpoint_count = orbitals.shape[0]
    group_count = screening.shape[0]
    group_ids = jnp.arange(group_count, dtype=jnp.int32)[:, None]
    second_k = ((pairs_k - group_ids) % kpoint_count).astype(jnp.int32)

    def per_group(inputs):
        screen_q, kpoint_a, kpoint_b = inputs
        orb_a = orbitals[kpoint_a].astype(jnp.float32)
        orb_b = orbitals[kpoint_b].astype(jnp.float32)
        pair_count = orb_a.shape[0]
        val_pairs = (orb_a[:, :NV, None, :] * orb_b[:, None, :NV, :]).astype(jnp.bfloat16)
        val_pairs = val_pairs.reshape(pair_count * NV * NV, NMU)
        cond_pairs = (orb_a[:, NV:, None, :] * orb_b[:, None, NV:, :]).astype(jnp.bfloat16)
        cond_pairs = cond_pairs.reshape(pair_count, NC * NC, NMU)
        screened = jnp.dot(val_pairs, screen_q, preferred_element_type=jnp.float32).astype(jnp.bfloat16)
        screened = screened.reshape(pair_count, NV * NV, NMU)
        return jnp.einsum("pan,pbn->pab", screened.astype(jnp.float32), cond_pairs.astype(jnp.float32))

    return lax.map(per_group, (screening, pairs_k, second_k))
```

```python
import jax
import jax.numpy as jnp
from jax import lax
from jax.sharding import PartitionSpec as P

NV = 16
NC = 32


def body(orbitals, screening, pairs_k):
    k_dev, orb_count, mu_cols = orbitals.shape
    group_count = lax.axis_size("pb")
    col_count = lax.axis_size("col")
    kpoint_count = k_dev * group_count
    group_index = lax.axis_index("pb")
    kpoint_a = pairs_k[0]
    kpoint_b = (kpoint_a - group_index) % kpoint_count
    pair_count = kpoint_a.shape[0]

    valence_all = lax.all_gather(orbitals[:, :NV, :], ("pb", "col"), axis=0, tiled=True)
    valence_all = jnp.transpose(
        valence_all.reshape(kpoint_count, col_count, NV, mu_cols), (0, 2, 1, 3)
    ).reshape(kpoint_count, NV, col_count * mu_cols)
    conduction_all = lax.all_gather(orbitals[:, NV:, :], "pb", axis=0, tiled=True)

    valence_a = jnp.take(valence_all, kpoint_a, axis=0).astype(jnp.float32)
    valence_b = jnp.take(valence_all, kpoint_b, axis=0).astype(jnp.float32)
    val_pairs = (valence_a[:, :, None, :] * valence_b[:, None, :, :]).astype(jnp.bfloat16)
    val_pairs = val_pairs.reshape(pair_count * NV * NV, col_count * mu_cols)
    screened = jnp.dot(val_pairs, screening[0], preferred_element_type=jnp.float32).astype(
        jnp.bfloat16
    )
    screened = screened.reshape(pair_count, NV * NV, mu_cols)

    cond_a = jnp.take(conduction_all, kpoint_a, axis=0).astype(jnp.float32)
    cond_b = jnp.take(conduction_all, kpoint_b, axis=0).astype(jnp.float32)
    cond_pairs = (cond_a[:, :, None, :] * cond_b[:, None, :, :]).astype(jnp.bfloat16)
    cond_pairs = cond_pairs.reshape(pair_count, NC * NC, mu_cols)
    partial_value = jnp.einsum(
        "pan,pbn->pab", screened, cond_pairs, preferred_element_type=jnp.float32
    )
    result = lax.psum_scatter(partial_value, "col", scatter_dimension=2, tiled=True)
    return result[None]


def solution(mesh):
    placed = (P("pb", None, "col"), P("pb", None, "col"), P("pb", None))
    return jax.shard_map(
        body, mesh=mesh, in_specs=placed, out_specs=P("pb", None, None, "col"), check_vma=False
    )
```

```python
import jax
import jax.numpy as jnp
from jax import lax
from jax.sharding import PartitionSpec as P

NV = 16
NC = 32


def swap(x, axis, bit):
    size = lax.axis_size(axis)
    return lax.ppermute(x, axis, [(i, i ^ bit) for i in range(size)])


def gather_col(mine):
    col_count = lax.axis_size("col")
    me = lax.axis_index("col")
    cur = mine[None]
    bit = col_count // 2
    while bit >= 1:
        got = swap(cur, "col", bit)
        low = (me & bit) == 0
        cur = jnp.where(low, jnp.stack([cur, got], 1), jnp.stack([got, cur], 1))
        cur = cur.reshape((-1,) + mine.shape)
        bit //= 2
    return cur


def scatter_sum_col(partial):
    col_count = lax.axis_size("col")
    me = lax.axis_index("col")
    width = partial.shape[-1] // col_count
    lead = partial.shape[:-1]
    cur = partial.reshape(lead + (col_count, width))
    bit = 1
    shift = 0
    while bit < col_count:
        parts = cur.shape[-2]
        cur = cur.reshape(lead + (parts // 2, 2, width))
        mine_bit = (me >> shift) & 1
        keep = lax.dynamic_index_in_dim(cur, mine_bit, len(lead) + 1, keepdims=False)
        send = lax.dynamic_index_in_dim(cur, 1 - mine_bit, len(lead) + 1, keepdims=False)
        cur = keep + swap(send, "col", bit)
        bit *= 2
        shift += 1
    return cur.reshape(lead + (width,))


def body(orbitals, screening, pairs_k):
    k_dev, orb_count, mu_cols = orbitals.shape
    group_count = lax.axis_size("pb")
    col_count = lax.axis_size("col")
    kpoint_count = k_dev * group_count
    group_index = lax.axis_index("pb")
    kpoint_a = pairs_k[0]
    kpoint_b = (kpoint_a - group_index) % kpoint_count
    pair_count = kpoint_a.shape[0]

    held = [orbitals]
    for s in range(1, group_count):
        held.append(
            lax.ppermute(orbitals, "pb", [(i, (i + s) % group_count) for i in range(group_count)])
        )
    held = jnp.concatenate(held, 0)

    def slot_of(k):
        return ((group_index - k // k_dev) % group_count) * k_dev + k % k_dev

    wanted = jnp.concatenate([slot_of(kpoint_a), slot_of(kpoint_b)])
    chosen = jnp.take(held, wanted, axis=0)

    valence = gather_col(chosen[:, :NV, :])
    valence = jnp.transpose(valence, (1, 2, 0, 3)).reshape(
        2 * pair_count, NV, col_count * mu_cols
    )
    valence_a = valence[:pair_count].astype(jnp.float32)
    valence_b = valence[pair_count:].astype(jnp.float32)
    val_pairs = (valence_a[:, :, None, :] * valence_b[:, None, :, :]).astype(jnp.bfloat16)
    val_pairs = val_pairs.reshape(pair_count * NV * NV, col_count * mu_cols)
    screened = jnp.dot(val_pairs, screening[0], preferred_element_type=jnp.float32).astype(
        jnp.bfloat16
    )
    screened = screened.reshape(pair_count, NV * NV, mu_cols)

    conduction = chosen[:, NV:, :].astype(jnp.float32)
    cond_pairs = (
        conduction[:pair_count, :, None, :] * conduction[pair_count:, None, :, :]
    ).astype(jnp.bfloat16)
    cond_pairs = cond_pairs.reshape(pair_count, NC * NC, mu_cols)
    partial_value = jnp.einsum(
        "pan,pbn->pab", screened, cond_pairs, preferred_element_type=jnp.float32
    )
    return scatter_sum_col(partial_value)[None]


def solution(mesh):
    placed = (P("pb", None, "col"), P("pb", None, "col"), P("pb", None))
    return jax.shard_map(
        body, mesh=mesh, in_specs=placed, out_specs=P("pb", None, None, "col"), check_vma=False
    )
```

```python
import jax
import jax.numpy as jnp
from jax import lax
from jax.sharding import PartitionSpec as P

NV = 16
NC = 32
PAIR_CHUNKS = 2


def swap(x, axis, bit):
    size = lax.axis_size(axis)
    return lax.ppermute(x, axis, [(i, i ^ bit) for i in range(size)])


def gather_col(mine):
    col_count = lax.axis_size("col")
    me = lax.axis_index("col")
    cur = mine[None]
    bit = col_count // 2
    while bit >= 1:
        got = swap(cur, "col", bit)
        low = (me & bit) == 0
        cur = jnp.where(low, jnp.stack([cur, got], 1), jnp.stack([got, cur], 1))
        cur = cur.reshape((-1,) + mine.shape)
        bit //= 2
    return cur


def scatter_sum_col(own_block, last_swap):
    col_count = lax.axis_size("col")
    acc = {}
    extra = None
    bit = 1
    while bit < col_count:
        deltas = [d for d in range(col_count) if d & bit and d % bit == 0]
        send = []
        for d in deltas:
            value = acc.pop(d) if d in acc else own_block(d)
            send.append(value)
        send = jnp.stack(send)
        if bit * 2 >= col_count:
            got, extra = last_swap(send, bit)
        else:
            got = swap(send, "col", bit)
        for i, d in enumerate(deltas):
            kept = d ^ bit
            base = acc.pop(kept) if kept in acc else own_block(kept)
            acc[kept] = base + got[i]
        bit *= 2
    return (acc[0] if 0 in acc else own_block(0)), extra


def screened_of(valence_a, valence_b, screening):
    chunk = valence_a.shape[0]
    valence_a = valence_a.astype(jnp.float32)
    valence_b = valence_b.astype(jnp.float32)
    val_pairs = (valence_a[:, :, None, :] * valence_b[:, None, :, :]).astype(jnp.bfloat16)
    val_pairs = val_pairs.reshape(chunk * NV * NV, valence_a.shape[2])
    screened = jnp.dot(val_pairs, screening, preferred_element_type=jnp.float32).astype(
        jnp.bfloat16
    )
    return screened.reshape(chunk, NV * NV, screening.shape[1])


def body(orbitals, screening, pairs_k):
    k_dev, orb_count, mu_cols = orbitals.shape
    group_count = lax.axis_size("pb")
    col_count = lax.axis_size("col")
    kpoint_count = k_dev * group_count
    group_index = lax.axis_index("pb")
    col_index = lax.axis_index("col")
    kpoint_a = pairs_k[0]
    kpoint_b = (kpoint_a - group_index) % kpoint_count
    pair_count = kpoint_a.shape[0]

    held = [orbitals]
    for s in range(1, group_count):
        held.append(
            lax.ppermute(orbitals, "pb", [(i, (i + s) % group_count) for i in range(group_count)])
        )
    held = jnp.concatenate(held, 0)

    def slot_of(k):
        return ((group_index - k // k_dev) % group_count) * k_dev + k % k_dev

    wanted = jnp.concatenate([slot_of(kpoint_a), slot_of(kpoint_b)])
    chosen = jnp.take(held, wanted, axis=0)

    valence = gather_col(chosen[:, :NV, :])
    valence = jnp.transpose(valence, (1, 2, 0, 3)).reshape(
        2 * pair_count, NV, col_count * mu_cols
    )
    conduction = chosen[:, NV:, :].astype(jnp.float32)
    rows_per_block = NC // col_count
    chunk = pair_count // PAIR_CHUNKS
    starts = list(range(0, pair_count, chunk))

    def valence_of(first):
        return valence[first : first + chunk], valence[pair_count + first : pair_count + first + chunk]

    results = []
    screened = screened_of(*valence_of(starts[0]), screening[0])
    for n_chunk, first in enumerate(starts):
        cond_a = conduction[first : first + chunk]
        cond_b = conduction[pair_count + first : pair_count + first + chunk]

        def own_block(delta, screened=screened, cond_a=cond_a, cond_b=cond_b):
            block = col_index ^ delta
            rows = lax.dynamic_slice_in_dim(cond_a, block * rows_per_block, rows_per_block, 1)
            cond_pairs = (rows[:, :, None, :] * cond_b[:, None, :, :]).astype(jnp.bfloat16)
            cond_pairs = cond_pairs.reshape(chunk, rows_per_block * NC, mu_cols)
            return jnp.einsum(
                "pan,pbn->pab", screened, cond_pairs, preferred_element_type=jnp.float32
            )

        def last_swap(send, bit):
            return swap(send, "col", bit), None

        summed, _ = scatter_sum_col(own_block, last_swap)
        results.append(summed)
        if n_chunk + 1 < len(starts):
            screened = screened_of(*valence_of(starts[n_chunk + 1]), screening[0])
    return jnp.concatenate(results, 0)[None]


def solution(mesh):
    placed = (P("pb", None, "col"), P("pb", None, "col"), P("pb", None))
    return jax.shard_map(
        body, mesh=mesh, in_specs=placed, out_specs=P("pb", None, None, "col"), check_vma=False
    )
```

```python
import jax
import jax.numpy as jnp
from jax import lax
from jax.sharding import PartitionSpec as P

NV = 16
NC = 32
PAIR_CHUNKS = 2


def swap(x, axis, bit):
    size = lax.axis_size(axis)
    return lax.ppermute(x, axis, [(i, i ^ bit) for i in range(size)])


def gather_axis(mine, axis):
    count = lax.axis_size(axis)
    me = lax.axis_index(axis)
    cur = mine[None]
    bit = count // 2
    while bit >= 1:
        got = swap(cur, axis, bit)
        low = (me & bit) == 0
        cur = jnp.where(low, jnp.stack([cur, got], 1), jnp.stack([got, cur], 1))
        cur = cur.reshape((-1,) + mine.shape)
        bit //= 2
    return cur


def scatter_sum_col(own_block, last_swap):
    col_count = lax.axis_size("col")
    acc = {}
    extra = None
    bit = 1
    while bit < col_count:
        deltas = [d for d in range(col_count) if d & bit and d % bit == 0]
        send = []
        for d in deltas:
            value = acc.pop(d) if d in acc else own_block(d)
            send.append(value)
        send = jnp.stack(send)
        if bit * 2 >= col_count:
            got, extra = last_swap(send, bit)
        else:
            got = swap(send, "col", bit)
        for i, d in enumerate(deltas):
            kept = d ^ bit
            base = acc.pop(kept) if kept in acc else own_block(kept)
            acc[kept] = base + got[i]
        bit *= 2
    return (acc[0] if 0 in acc else own_block(0)), extra


def screened_of(valence_a, valence_b, screening):
    chunk = valence_a.shape[0]
    valence_a = valence_a.astype(jnp.float32)
    valence_b = valence_b.astype(jnp.float32)
    val_pairs = (valence_a[:, :, None, :] * valence_b[:, None, :, :]).astype(jnp.bfloat16)
    val_pairs = val_pairs.reshape(chunk * NV * NV, valence_a.shape[2])
    screened = jnp.dot(val_pairs, screening, preferred_element_type=jnp.float32).astype(
        jnp.bfloat16
    )
    return screened.reshape(chunk, NV * NV, screening.shape[1])


def body(orbitals, screening, pairs_k):
    k_dev, orb_count, mu_cols = orbitals.shape
    group_count = lax.axis_size("pb")
    col_count = lax.axis_size("col")
    kpoint_count = k_dev * group_count
    group_index = lax.axis_index("pb")
    col_index = lax.axis_index("col")
    kpoint_a = pairs_k[0]
    kpoint_b = (kpoint_a - group_index) % kpoint_count
    pair_count = kpoint_a.shape[0]

    held = gather_axis(orbitals, "pb").reshape(kpoint_count, orb_count, mu_cols)
    wanted = jnp.concatenate([kpoint_a, kpoint_b])
    chosen = jnp.take(held, wanted, axis=0)

    valence = gather_axis(chosen[:, :NV, :], "col")
    valence = jnp.transpose(valence, (1, 2, 0, 3)).reshape(
        2 * pair_count, NV, col_count * mu_cols
    )
    conduction = chosen[:, NV:, :].astype(jnp.float32)
    rows_per_block = NC // col_count
    chunk = pair_count // PAIR_CHUNKS
    starts = list(range(0, pair_count, chunk))

    def valence_of(first):
        return valence[first : first + chunk], valence[pair_count + first : pair_count + first + chunk]

    results = []
    screened = screened_of(*valence_of(starts[0]), screening[0])
    for n_chunk, first in enumerate(starts):
        cond_a = conduction[first : first + chunk]
        cond_b = conduction[pair_count + first : pair_count + first + chunk]

        def own_block(delta, screened=screened, cond_a=cond_a, cond_b=cond_b):
            block = col_index ^ delta
            rows = lax.dynamic_slice_in_dim(cond_a, block * rows_per_block, rows_per_block, 1)
            cond_pairs = (rows[:, :, None, :] * cond_b[:, None, :, :]).astype(jnp.bfloat16)
            cond_pairs = cond_pairs.reshape(chunk, rows_per_block * NC, mu_cols)
            return jnp.einsum(
                "pan,pbn->pab", screened, cond_pairs, preferred_element_type=jnp.float32
            )

        def last_swap(send, bit):
            return swap(send, "col", bit), None

        summed, _ = scatter_sum_col(own_block, last_swap)
        results.append(summed)
        if n_chunk + 1 < len(starts):
            screened = screened_of(*valence_of(starts[n_chunk + 1]), screening[0])
    return jnp.concatenate(results, 0)[None]


def solution(mesh):
    placed = (P("pb", None, "col"), P("pb", None, "col"), P("pb", None))
    return jax.shard_map(
        body, mesh=mesh, in_specs=placed, out_specs=P("pb", None, None, "col"), check_vma=False
    )
```

```python
import jax
import jax.numpy as jnp
from jax import lax
from jax.sharding import PartitionSpec as P

NV = 16
NC = 32
PAIR_CHUNKS = 2


def swap(x, axis, bit):
    size = lax.axis_size(axis)
    return lax.ppermute(x, axis, [(i, i ^ bit) for i in range(size)])


def gather_axis(mine, axis):
    count = lax.axis_size(axis)
    me = lax.axis_index(axis)
    cur = mine[None]
    bit = count // 2
    while bit >= 1:
        got = swap(cur, axis, bit)
        low = (me & bit) == 0
        cur = jnp.where(low, jnp.stack([cur, got], 1), jnp.stack([got, cur], 1))
        cur = cur.reshape((-1,) + mine.shape)
        bit //= 2
    return cur


def scatter_sum_col(own_block, last_swap):
    col_count = lax.axis_size("col")
    acc = {}
    extra = None
    bit = 1
    while bit < col_count:
        deltas = [d for d in range(col_count) if d & bit and d % bit == 0]
        send = []
        for d in deltas:
            value = acc.pop(d) if d in acc else own_block(d)
            send.append(value)
        send = jnp.stack(send)
        if bit * 2 >= col_count:
            got, extra = last_swap(send, bit)
        else:
            got = swap(send, "col", bit)
        for i, d in enumerate(deltas):
            kept = d ^ bit
            base = acc.pop(kept) if kept in acc else own_block(kept)
            acc[kept] = base + got[i]
        bit *= 2
    return (acc[0] if 0 in acc else own_block(0)), extra


def screened_of(valence_a, valence_b, screening):
    chunk = valence_a.shape[0]
    valence_a = valence_a.astype(jnp.float32)
    valence_b = valence_b.astype(jnp.float32)
    val_pairs = (valence_a[:, :, None, :] * valence_b[:, None, :, :]).astype(jnp.bfloat16)
    val_pairs = val_pairs.reshape(chunk * NV * NV, valence_a.shape[2])
    screened = jnp.dot(val_pairs, screening, preferred_element_type=jnp.float32).astype(
        jnp.bfloat16
    )
    return screened.reshape(chunk, NV * NV, screening.shape[1])


def body(orbitals, screening, pairs_k):
    k_dev, orb_count, mu_cols = orbitals.shape
    group_count = lax.axis_size("pb")
    col_count = lax.axis_size("col")
    kpoint_count = k_dev * group_count
    group_index = lax.axis_index("pb")
    col_index = lax.axis_index("col")
    kpoint_a = pairs_k[0]
    kpoint_b = (kpoint_a - group_index) % kpoint_count
    pair_count = kpoint_a.shape[0]

    held = gather_axis(orbitals, "pb").reshape(kpoint_count, orb_count, mu_cols)
    wanted = jnp.concatenate([kpoint_a, kpoint_b])
    chosen = jnp.take(held, wanted, axis=0)

    valence = gather_axis(chosen[:, :NV, :], "col")
    valence = jnp.transpose(valence, (1, 2, 0, 3)).reshape(
        2 * pair_count, NV, col_count * mu_cols
    )
    conduction = chosen[:, NV:, :].astype(jnp.float32)
    rows_per_block = NC // col_count
    chunk = pair_count // PAIR_CHUNKS
    starts = list(range(0, pair_count, chunk))

    def valence_of(first):
        return valence[first : first + chunk], valence[pair_count + first : pair_count + first + chunk]

    results = []
    screened = screened_of(*valence_of(starts[0]), screening[0])
    for n_chunk, first in enumerate(starts):
        cond_a = conduction[first : first + chunk]
        cond_b = conduction[pair_count + first : pair_count + first + chunk]

        def own_block(delta, screened=screened, cond_a=cond_a, cond_b=cond_b):
            block = col_index ^ delta
            rows = lax.dynamic_slice_in_dim(cond_a, block * rows_per_block, rows_per_block, 1)
            cond_pairs = (rows[:, :, None, :] * cond_b[:, None, :, :]).astype(jnp.bfloat16)
            cond_pairs = cond_pairs.reshape(chunk, rows_per_block * NC, mu_cols)
            return jnp.einsum(
                "pan,pbn->pab", screened, cond_pairs, preferred_element_type=jnp.float32
            )

        def last_swap(send, bit):
            got = swap(send.astype(jnp.bfloat16), "col", bit)
            return got.astype(jnp.float32), None

        summed, _ = scatter_sum_col(own_block, last_swap)
        results.append(summed)
        if n_chunk + 1 < len(starts):
            screened = screened_of(*valence_of(starts[n_chunk + 1]), screening[0])
    return jnp.concatenate(results, 0)[None]


def solution(mesh):
    placed = (P("pb", None, "col"), P("pb", None, "col"), P("pb", None))
    return jax.shard_map(
        body, mesh=mesh, in_specs=placed, out_specs=P("pb", None, None, "col"), check_vma=False
    )
```

```python
import jax
import jax.numpy as jnp
from jax import lax
from jax.sharding import PartitionSpec as P

NV = 16
NC = 32
PAIR_CHUNKS = 2


def swap(x, axis, bit):
    size = lax.axis_size(axis)
    return lax.ppermute(x, axis, [(i, i ^ bit) for i in range(size)])


def gather_axis(mine, axis):
    count = lax.axis_size(axis)
    me = lax.axis_index(axis)
    cur = mine[None]
    bit = count // 2
    while bit >= 1:
        got = swap(cur, axis, bit)
        low = (me & bit) == 0
        cur = jnp.where(low, jnp.stack([cur, got], 1), jnp.stack([got, cur], 1))
        cur = cur.reshape((-1,) + mine.shape)
        bit //= 2
    return cur


def scatter_sum_col(own_block, last_swap):
    col_count = lax.axis_size("col")
    acc = {}
    extra = None
    bit = 1
    while bit < col_count:
        deltas = [d for d in range(col_count) if d & bit and d % bit == 0]
        send = []
        for d in deltas:
            value = acc.pop(d) if d in acc else own_block(d)
            send.append(value)
        send = jnp.stack(send)
        if bit * 2 >= col_count:
            got, extra = last_swap(send, bit)
        else:
            got = swap(send, "col", bit)
        for i, d in enumerate(deltas):
            kept = d ^ bit
            base = acc.pop(kept) if kept in acc else own_block(kept)
            acc[kept] = base + got[i]
        bit *= 2
    return (acc[0] if 0 in acc else own_block(0)), extra


def screened_of(valence_a, valence_b, screening):
    chunk = valence_a.shape[0]
    valence_a = valence_a.astype(jnp.float32)
    valence_b = valence_b.astype(jnp.float32)
    val_pairs = (valence_a[:, :, None, :] * valence_b[:, None, :, :]).astype(jnp.bfloat16)
    val_pairs = val_pairs.reshape(chunk * NV * NV, valence_a.shape[2])
    screened = jnp.dot(val_pairs, screening, preferred_element_type=jnp.float32).astype(
        jnp.bfloat16
    )
    return screened.reshape(chunk, NV * NV, screening.shape[1])


def body(orbitals, screening, pairs_k):
    k_dev, orb_count, mu_cols = orbitals.shape
    group_count = lax.axis_size("pb")
    col_count = lax.axis_size("col")
    kpoint_count = k_dev * group_count
    group_index = lax.axis_index("pb")
    col_index = lax.axis_index("col")
    kpoint_a = pairs_k[0]
    kpoint_b = (kpoint_a - group_index) % kpoint_count
    pair_count = kpoint_a.shape[0]

    held = gather_axis(orbitals, "pb").reshape(kpoint_count, orb_count, mu_cols)
    wanted = jnp.concatenate([kpoint_a, kpoint_b])
    chosen = jnp.take(held, wanted, axis=0)

    valence = gather_axis(chosen[:, :NV, :], "col")
    valence = jnp.transpose(valence, (1, 2, 0, 3)).reshape(
        2 * pair_count, NV, col_count * mu_cols
    )
    conduction = chosen[:, NV:, :].astype(jnp.float32)
    rows_per_block = NC // col_count
    chunk = pair_count // PAIR_CHUNKS
    starts = list(range(0, pair_count, chunk))

    def valence_of(first):
        return valence[first : first + chunk], valence[pair_count + first : pair_count + first + chunk]

    results = []
    screened = screened_of(*valence_of(starts[0]), screening[0])
    for n_chunk, first in enumerate(starts):
        cond_a = conduction[first : first + chunk]
        cond_b = conduction[pair_count + first : pair_count + first + chunk]

        def own_block(delta, screened=screened, cond_a=cond_a, cond_b=cond_b):
            block = col_index ^ delta
            rows = lax.dynamic_slice_in_dim(cond_a, block * rows_per_block, rows_per_block, 1)
            cond_pairs = (rows[:, :, None, :] * cond_b[:, None, :, :]).astype(jnp.bfloat16)
            cond_pairs = cond_pairs.reshape(chunk, rows_per_block * NC, mu_cols)
            return jnp.einsum(
                "pan,pbn->pab", screened, cond_pairs, preferred_element_type=jnp.float32
            )

        following = valence_of(starts[n_chunk + 1]) if n_chunk + 1 < len(starts) else None

        def last_swap(send, bit, following=following):
            send = send.astype(jnp.bfloat16)
            if following is None:
                return swap(send, "col", bit).astype(jnp.float32), None
            send, following = lax.optimization_barrier((send, following))
            got = swap(send, "col", bit)
            screened_next = screened_of(*following, screening[0])
            got, screened_next = lax.optimization_barrier((got, screened_next))
            return got.astype(jnp.float32), screened_next

        summed, screened = scatter_sum_col(own_block, last_swap)
        results.append(summed)
    return jnp.concatenate(results, 0)[None]


def solution(mesh):
    placed = (P("pb", None, "col"), P("pb", None, "col"), P("pb", None))
    return jax.shard_map(
        body, mesh=mesh, in_specs=placed, out_specs=P("pb", None, None, "col"), check_vma=False
    )
```

```python
import jax
import jax.numpy as jnp
from jax import lax
from jax.sharding import PartitionSpec as P

NV = 16
NC = 32
PAIR_CHUNKS = 2


def swap(x, axis, bit):
    size = lax.axis_size(axis)
    return lax.ppermute(x, axis, [(i, i ^ bit) for i in range(size)])


def gather_axis(mine, axis):
    count = lax.axis_size(axis)
    me = lax.axis_index(axis)
    cur = mine[None]
    bit = count // 2
    while bit >= 1:
        got = swap(cur, axis, bit)
        low = (me & bit) == 0
        cur = jnp.where(low, jnp.stack([cur, got], 1), jnp.stack([got, cur], 1))
        cur = cur.reshape((-1,) + mine.shape)
        bit //= 2
    return cur


def scatter_sum_col(own_block, last_swap):
    col_count = lax.axis_size("col")
    acc = {}
    extra = None
    bit = 1
    while bit < col_count:
        deltas = [d for d in range(col_count) if d & bit and d % bit == 0]
        send = []
        for d in deltas:
            value = acc.pop(d) if d in acc else own_block(d)
            send.append(value)
        send = jnp.stack(send)
        if bit * 2 >= col_count:
            got, extra = last_swap(send, bit)
        else:
            got = swap(send, "col", bit)
        for i, d in enumerate(deltas):
            kept = d ^ bit
            base = acc.pop(kept) if kept in acc else own_block(kept)
            acc[kept] = base + got[i]
        bit *= 2
    return (acc[0] if 0 in acc else own_block(0)), extra


def screened_of(valence_a, valence_b, screening):
    chunk = valence_a.shape[0]
    valence_a = valence_a.astype(jnp.float32)
    valence_b = valence_b.astype(jnp.float32)
    val_pairs = (valence_a[:, :, None, :] * valence_b[:, None, :, :]).astype(jnp.bfloat16)
    val_pairs = val_pairs.reshape(chunk * NV * NV, valence_a.shape[2])
    screened = jnp.dot(val_pairs, screening, preferred_element_type=jnp.float32).astype(
        jnp.bfloat16
    )
    return screened.reshape(chunk, NV * NV, screening.shape[1])


def body(orbitals, screening, pairs_k):
    k_dev, orb_count, mu_cols = orbitals.shape
    group_count = lax.axis_size("pb")
    col_count = lax.axis_size("col")
    kpoint_count = k_dev * group_count
    group_index = lax.axis_index("pb")
    col_index = lax.axis_index("col")
    kpoint_a = pairs_k[0]
    kpoint_b = (kpoint_a - group_index) % kpoint_count
    pair_count = kpoint_a.shape[0]

    wanted = jnp.concatenate([kpoint_a, kpoint_b])
    held_valence = gather_axis(orbitals[:, :NV, :], "pb").reshape(kpoint_count, NV, mu_cols)
    held_conduction = gather_axis(orbitals[:, NV:, :], "pb").reshape(
        kpoint_count, orb_count - NV, mu_cols
    )

    valence = gather_axis(jnp.take(held_valence, wanted, axis=0), "col")
    valence = jnp.transpose(valence, (1, 2, 0, 3)).reshape(
        2 * pair_count, NV, col_count * mu_cols
    )
    conduction = jnp.take(held_conduction, wanted, axis=0).astype(jnp.float32)
    rows_per_block = NC // col_count
    chunk = pair_count // PAIR_CHUNKS
    starts = list(range(0, pair_count, chunk))

    def valence_of(first):
        return valence[first : first + chunk], valence[pair_count + first : pair_count + first + chunk]

    results = []
    screened = screened_of(*valence_of(starts[0]), screening[0])
    for n_chunk, first in enumerate(starts):
        cond_a = conduction[first : first + chunk]
        cond_b = conduction[pair_count + first : pair_count + first + chunk]

        def own_block(delta, screened=screened, cond_a=cond_a, cond_b=cond_b):
            block = col_index ^ delta
            rows = lax.dynamic_slice_in_dim(cond_a, block * rows_per_block, rows_per_block, 1)
            cond_pairs = (rows[:, :, None, :] * cond_b[:, None, :, :]).astype(jnp.bfloat16)
            cond_pairs = cond_pairs.reshape(chunk, rows_per_block * NC, mu_cols)
            return jnp.einsum(
                "pan,pbn->pab", screened, cond_pairs, preferred_element_type=jnp.float32
            )

        def last_swap(send, bit):
            got = swap(send.astype(jnp.bfloat16), "col", bit)
            return got.astype(jnp.float32), None

        summed, _ = scatter_sum_col(own_block, last_swap)
        results.append(summed)
        if n_chunk + 1 < len(starts):
            screened = screened_of(*valence_of(starts[n_chunk + 1]), screening[0])
    return jnp.concatenate(results, 0)[None]


def solution(mesh):
    placed = (P("pb", None, "col"), P("pb", None, "col"), P("pb", None))
    return jax.shard_map(
        body, mesh=mesh, in_specs=placed, out_specs=P("pb", None, None, "col"), check_vma=False
    )
```

```python
import jax
import jax.numpy as jnp
from jax import lax
from jax.sharding import PartitionSpec as P

NV = 16
NC = 32
PAIR_CHUNKS = 2


def swap(x, axis, bit):
    size = lax.axis_size(axis)
    return lax.ppermute(x, axis, [(i, i ^ bit) for i in range(size)])


def gather_axis(mine, axis):
    count = lax.axis_size(axis)
    me = lax.axis_index(axis)
    cur = mine[None]
    bit = count // 2
    while bit >= 1:
        got = swap(cur, axis, bit)
        low = (me & bit) == 0
        cur = jnp.where(low, jnp.stack([cur, got], 1), jnp.stack([got, cur], 1))
        cur = cur.reshape((-1,) + mine.shape)
        bit //= 2
    return cur


def scatter_sum_col(own_block, last_swap):
    col_count = lax.axis_size("col")
    acc = {}
    extra = None
    bit = 1
    while bit < col_count:
        deltas = [d for d in range(col_count) if d & bit and d % bit == 0]
        send = []
        for d in deltas:
            value = acc.pop(d) if d in acc else own_block(d)
            send.append(value)
        send = jnp.stack(send)
        if bit * 2 >= col_count:
            got, extra = last_swap(send, bit)
        else:
            got = swap(send, "col", bit)
        for i, d in enumerate(deltas):
            kept = d ^ bit
            base = acc.pop(kept) if kept in acc else own_block(kept)
            acc[kept] = base + got[i]
        bit *= 2
    return (acc[0] if 0 in acc else own_block(0)), extra


def screened_of(valence_a, valence_b, screening):
    chunk = valence_a.shape[0]
    valence_a = valence_a.astype(jnp.float32)
    valence_b = valence_b.astype(jnp.float32)
    val_pairs = (valence_a[:, :, None, :] * valence_b[:, None, :, :]).astype(jnp.bfloat16)
    val_pairs = val_pairs.reshape(chunk * NV * NV, valence_a.shape[2])
    screened = jnp.dot(val_pairs, screening, preferred_element_type=jnp.float32).astype(
        jnp.bfloat16
    )
    return screened.reshape(chunk, NV * NV, screening.shape[1])


def body(orbitals, screening, pairs_k):
    k_dev, orb_count, mu_cols = orbitals.shape
    group_count = lax.axis_size("pb")
    col_count = lax.axis_size("col")
    kpoint_count = k_dev * group_count
    group_index = lax.axis_index("pb")
    col_index = lax.axis_index("col")
    kpoint_a = pairs_k[0]
    kpoint_b = (kpoint_a - group_index) % kpoint_count
    pair_count = kpoint_a.shape[0]

    wanted = jnp.concatenate([kpoint_a, kpoint_b])
    held_valence = gather_axis(orbitals[:, :NV, :], "pb").reshape(kpoint_count, NV, mu_cols)
    held_conduction = gather_axis(orbitals[:, NV:, :], "pb").reshape(
        kpoint_count, orb_count - NV, mu_cols
    )

    valence = gather_axis(jnp.take(held_valence, wanted, axis=0), "col")
    valence = jnp.transpose(valence, (1, 2, 0, 3)).reshape(
        2 * pair_count, NV, col_count * mu_cols
    )
    valence = lax.optimization_barrier(valence)
    conduction = jnp.take(held_conduction, wanted, axis=0).astype(jnp.float32)
    rows_per_block = NC // col_count
    chunk = pair_count // PAIR_CHUNKS
    starts = list(range(0, pair_count, chunk))

    def valence_of(first):
        return valence[first : first + chunk], valence[pair_count + first : pair_count + first + chunk]

    results = []
    screened = screened_of(*valence_of(starts[0]), screening[0])
    for n_chunk, first in enumerate(starts):
        cond_a = conduction[first : first + chunk]
        cond_b = conduction[pair_count + first : pair_count + first + chunk]

        def own_block(delta, screened=screened, cond_a=cond_a, cond_b=cond_b):
            block = col_index ^ delta
            rows = lax.dynamic_slice_in_dim(cond_a, block * rows_per_block, rows_per_block, 1)
            cond_pairs = (rows[:, :, None, :] * cond_b[:, None, :, :]).astype(jnp.bfloat16)
            cond_pairs = cond_pairs.reshape(chunk, rows_per_block * NC, mu_cols)
            return jnp.einsum(
                "pan,pbn->pab", screened, cond_pairs, preferred_element_type=jnp.float32
            )

        def last_swap(send, bit):
            got = swap(send.astype(jnp.bfloat16), "col", bit)
            return got.astype(jnp.float32), None

        summed, _ = scatter_sum_col(own_block, last_swap)
        results.append(summed)
        if n_chunk + 1 < len(starts):
            screened = screened_of(*valence_of(starts[n_chunk + 1]), screening[0])
    return jnp.concatenate(results, 0)[None]


def solution(mesh):
    placed = (P("pb", None, "col"), P("pb", None, "col"), P("pb", None))
    return jax.shard_map(
        body, mesh=mesh, in_specs=placed, out_specs=P("pb", None, None, "col"), check_vma=False
    )
```

```python
import jax
import jax.numpy as jnp
from jax import lax
from jax.sharding import PartitionSpec as P

NV = 16
NC = 32
PAIR_CHUNKS = 2


def swap(x, axis, bit):
    size = lax.axis_size(axis)
    return lax.ppermute(x, axis, [(i, i ^ bit) for i in range(size)])


def gather_axis(mine, axis):
    count = lax.axis_size(axis)
    me = lax.axis_index(axis)
    cur = mine[None]
    bit = count // 2
    while bit >= 1:
        got = swap(cur, axis, bit)
        low = (me & bit) == 0
        cur = jnp.where(low, jnp.stack([cur, got], 1), jnp.stack([got, cur], 1))
        cur = cur.reshape((-1,) + mine.shape)
        bit //= 2
    return cur


def scatter_sum_col(own_block, last_swap):
    col_count = lax.axis_size("col")
    acc = {}
    extra = None
    bit = 1
    while bit < col_count:
        deltas = [d for d in range(col_count) if d & bit and d % bit == 0]
        send = []
        for d in deltas:
            value = acc.pop(d) if d in acc else own_block(d)
            send.append(value)
        send = jnp.stack(send)
        if bit * 2 >= col_count:
            got, extra = last_swap(send, bit)
        else:
            got = swap(send, "col", bit)
        for i, d in enumerate(deltas):
            kept = d ^ bit
            base = acc.pop(kept) if kept in acc else own_block(kept)
            acc[kept] = base + got[i]
        bit *= 2
    return (acc[0] if 0 in acc else own_block(0)), extra


def screened_of(valence_a, valence_b, screening):
    col_count, chunk, _, mu_cols = valence_a.shape
    valence_a = valence_a.astype(jnp.float32)
    valence_b = valence_b.astype(jnp.float32)
    val_pairs = (valence_a[:, :, :, None, :] * valence_b[:, :, None, :, :]).astype(jnp.bfloat16)
    val_pairs = val_pairs.reshape(col_count, chunk * NV * NV, mu_cols)
    screen = screening.reshape(col_count, mu_cols, screening.shape[1])
    screened = lax.dot_general(
        val_pairs, screen, (((0, 2), (0, 1)), ((), ())), preferred_element_type=jnp.float32
    ).astype(jnp.bfloat16)
    return screened.reshape(chunk, NV * NV, screening.shape[1])


def body(orbitals, screening, pairs_k):
    k_dev, orb_count, mu_cols = orbitals.shape
    group_count = lax.axis_size("pb")
    col_count = lax.axis_size("col")
    kpoint_count = k_dev * group_count
    group_index = lax.axis_index("pb")
    col_index = lax.axis_index("col")
    kpoint_a = pairs_k[0]
    kpoint_b = (kpoint_a - group_index) % kpoint_count
    pair_count = kpoint_a.shape[0]

    wanted = jnp.concatenate([kpoint_a, kpoint_b])
    held_valence = gather_axis(orbitals[:, :NV, :], "pb").reshape(kpoint_count, NV, mu_cols)
    held_conduction = gather_axis(orbitals[:, NV:, :], "pb").reshape(
        kpoint_count, orb_count - NV, mu_cols
    )

    valence = gather_axis(jnp.take(held_valence, wanted, axis=0), "col")
    conduction = jnp.take(held_conduction, wanted, axis=0).astype(jnp.float32)
    rows_per_block = NC // col_count
    chunk = pair_count // PAIR_CHUNKS
    starts = list(range(0, pair_count, chunk))

    def valence_of(first):
        return (
            valence[:, first : first + chunk],
            valence[:, pair_count + first : pair_count + first + chunk],
        )

    results = []
    screened = screened_of(*valence_of(starts[0]), screening[0])
    for n_chunk, first in enumerate(starts):
        cond_a = conduction[first : first + chunk]
        cond_b = conduction[pair_count + first : pair_count + first + chunk]

        def own_block(delta, screened=screened, cond_a=cond_a, cond_b=cond_b):
            block = col_index ^ delta
            rows = lax.dynamic_slice_in_dim(cond_a, block * rows_per_block, rows_per_block, 1)
            cond_pairs = (rows[:, :, None, :] * cond_b[:, None, :, :]).astype(jnp.bfloat16)
            cond_pairs = cond_pairs.reshape(chunk, rows_per_block * NC, mu_cols)
            return jnp.einsum(
                "pan,pbn->pab", screened, cond_pairs, preferred_element_type=jnp.float32
            )

        def last_swap(send, bit):
            got = swap(send.astype(jnp.bfloat16), "col", bit)
            return got.astype(jnp.float32), None

        summed, _ = scatter_sum_col(own_block, last_swap)
        results.append(summed)
        if n_chunk + 1 < len(starts):
            screened = screened_of(*valence_of(starts[n_chunk + 1]), screening[0])
    return jnp.concatenate(results, 0)[None]


def solution(mesh):
    placed = (P("pb", None, "col"), P("pb", None, "col"), P("pb", None))
    return jax.shard_map(
        body, mesh=mesh, in_specs=placed, out_specs=P("pb", None, None, "col"), check_vma=False
    )
```

```python
import jax
import jax.numpy as jnp
from jax import lax
from jax.sharding import PartitionSpec as P

NV = 16
NC = 32
PAIR_CHUNKS = 1


def swap(x, axis, bit):
    size = lax.axis_size(axis)
    return lax.ppermute(x, axis, [(i, i ^ bit) for i in range(size)])


def gather_axis(mine, axis):
    count = lax.axis_size(axis)
    me = lax.axis_index(axis)
    cur = mine[None]
    bit = count // 2
    while bit >= 1:
        got = swap(cur, axis, bit)
        low = (me & bit) == 0
        cur = jnp.where(low, jnp.stack([cur, got], 1), jnp.stack([got, cur], 1))
        cur = cur.reshape((-1,) + mine.shape)
        bit //= 2
    return cur


def scatter_sum_col(own_block, last_swap):
    col_count = lax.axis_size("col")
    acc = {}
    extra = None
    bit = 1
    while bit < col_count:
        deltas = [d for d in range(col_count) if d & bit and d % bit == 0]
        send = []
        for d in deltas:
            value = acc.pop(d) if d in acc else own_block(d)
            send.append(value)
        send = jnp.stack(send)
        if bit * 2 >= col_count:
            got, extra = last_swap(send, bit)
        else:
            got = swap(send, "col", bit)
        for i, d in enumerate(deltas):
            kept = d ^ bit
            base = acc.pop(kept) if kept in acc else own_block(kept)
            acc[kept] = base + got[i]
        bit *= 2
    return (acc[0] if 0 in acc else own_block(0)), extra


def screened_of(valence_a, valence_b, screening):
    col_count, chunk, _, mu_cols = valence_a.shape
    valence_a = valence_a.astype(jnp.float32)
    valence_b = valence_b.astype(jnp.float32)
    val_pairs = (valence_a[:, :, :, None, :] * valence_b[:, :, None, :, :]).astype(jnp.bfloat16)
    val_pairs = val_pairs.reshape(col_count, chunk * NV * NV, mu_cols)
    screen = screening.reshape(col_count, mu_cols, screening.shape[1])
    screened = lax.dot_general(
        val_pairs, screen, (((0, 2), (0, 1)), ((), ())), preferred_element_type=jnp.float32
    ).astype(jnp.bfloat16)
    return screened.reshape(chunk, NV * NV, screening.shape[1])


def body(orbitals, screening, pairs_k):
    k_dev, orb_count, mu_cols = orbitals.shape
    group_count = lax.axis_size("pb")
    col_count = lax.axis_size("col")
    kpoint_count = k_dev * group_count
    group_index = lax.axis_index("pb")
    col_index = lax.axis_index("col")
    kpoint_a = pairs_k[0]
    kpoint_b = (kpoint_a - group_index) % kpoint_count
    pair_count = kpoint_a.shape[0]

    wanted = jnp.concatenate([kpoint_a, kpoint_b])
    held_valence = gather_axis(orbitals[:, :NV, :], "pb").reshape(kpoint_count, NV, mu_cols)
    held_conduction = gather_axis(orbitals[:, NV:, :], "pb").reshape(
        kpoint_count, orb_count - NV, mu_cols
    )

    valence = gather_axis(jnp.take(held_valence, wanted, axis=0), "col")
    conduction = jnp.take(held_conduction, wanted, axis=0).astype(jnp.float32)
    rows_per_block = NC // col_count
    chunk = pair_count // PAIR_CHUNKS
    starts = list(range(0, pair_count, chunk))

    def valence_of(first):
        return (
            valence[:, first : first + chunk],
            valence[:, pair_count + first : pair_count + first + chunk],
        )

    results = []
    screened = screened_of(*valence_of(starts[0]), screening[0])
    for n_chunk, first in enumerate(starts):
        cond_a = conduction[first : first + chunk]
        cond_b = conduction[pair_count + first : pair_count + first + chunk]

        def own_block(delta, screened=screened, cond_a=cond_a, cond_b=cond_b):
            block = col_index ^ delta
            rows = lax.dynamic_slice_in_dim(cond_a, block * rows_per_block, rows_per_block, 1)
            cond_pairs = (rows[:, :, None, :] * cond_b[:, None, :, :]).astype(jnp.bfloat16)
            cond_pairs = cond_pairs.reshape(chunk, rows_per_block * NC, mu_cols)
            return jnp.einsum(
                "pan,pbn->pab", screened, cond_pairs, preferred_element_type=jnp.float32
            )

        def last_swap(send, bit):
            got = swap(send.astype(jnp.bfloat16), "col", bit)
            return got.astype(jnp.float32), None

        summed, _ = scatter_sum_col(own_block, last_swap)
        results.append(summed)
        if n_chunk + 1 < len(starts):
            screened = screened_of(*valence_of(starts[n_chunk + 1]), screening[0])
    return jnp.concatenate(results, 0)[None]


def solution(mesh):
    placed = (P("pb", None, "col"), P("pb", None, "col"), P("pb", None))
    return jax.shard_map(
        body, mesh=mesh, in_specs=placed, out_specs=P("pb", None, None, "col"), check_vma=False
    )
```

```python
import jax
import jax.numpy as jnp
from jax import lax
from jax.sharding import PartitionSpec as P

NV = 16
NC = 32
PAIR_CHUNKS = 2


def swap(x, axis, bit):
    size = lax.axis_size(axis)
    return lax.ppermute(x, axis, [(i, i ^ bit) for i in range(size)])


def gather_axis(mine, axis, tie=None):
    count = lax.axis_size(axis)
    me = lax.axis_index(axis)
    cur = mine[None]
    bit = count // 2
    while bit >= 1:
        got = swap(cur, axis, bit)
        if tie is not None and bit > 1:
            got, tie = lax.optimization_barrier((got, tie))
        low = (me & bit) == 0
        cur = jnp.where(low, jnp.stack([cur, got], 1), jnp.stack([got, cur], 1))
        cur = cur.reshape((-1,) + mine.shape)
        bit //= 2
    if tie is None:
        return cur
    return cur, tie


def scatter_sum_col(own_block, last_swap):
    col_count = lax.axis_size("col")
    acc = {}
    extra = None
    bit = 1
    while bit < col_count:
        deltas = [d for d in range(col_count) if d & bit and d % bit == 0]
        send = []
        for d in deltas:
            value = acc.pop(d) if d in acc else own_block(d)
            send.append(value)
        send = jnp.stack(send)
        if bit * 2 >= col_count:
            got, extra = last_swap(send, bit)
        else:
            got = swap(send, "col", bit)
        for i, d in enumerate(deltas):
            kept = d ^ bit
            base = acc.pop(kept) if kept in acc else own_block(kept)
            acc[kept] = base + got[i]
        bit *= 2
    return (acc[0] if 0 in acc else own_block(0)), extra


def screened_of(valence_a, valence_b, screening):
    col_count, chunk, _, mu_cols = valence_a.shape
    valence_a = valence_a.astype(jnp.float32)
    valence_b = valence_b.astype(jnp.float32)
    val_pairs = (valence_a[:, :, :, None, :] * valence_b[:, :, None, :, :]).astype(jnp.bfloat16)
    val_pairs = val_pairs.reshape(col_count, chunk * NV * NV, mu_cols)
    screen = screening.reshape(col_count, mu_cols, screening.shape[1])
    screened = lax.dot_general(
        val_pairs, screen, (((0, 2), (0, 1)), ((), ())), preferred_element_type=jnp.float32
    ).astype(jnp.bfloat16)
    return screened.reshape(chunk, NV * NV, screening.shape[1])


def body(orbitals, screening, pairs_k):
    k_dev, orb_count, mu_cols = orbitals.shape
    group_count = lax.axis_size("pb")
    col_count = lax.axis_size("col")
    kpoint_count = k_dev * group_count
    group_index = lax.axis_index("pb")
    col_index = lax.axis_index("col")
    kpoint_a = pairs_k[0]
    kpoint_b = (kpoint_a - group_index) % kpoint_count
    pair_count = kpoint_a.shape[0]

    wanted = jnp.concatenate([kpoint_a, kpoint_b])
    held_valence = gather_axis(orbitals[:, :NV, :], "pb").reshape(kpoint_count, NV, mu_cols)
    held_conduction = gather_axis(orbitals[:, NV:, :], "pb").reshape(
        kpoint_count, orb_count - NV, mu_cols
    )

    conduction = jnp.take(held_conduction, wanted, axis=0).astype(jnp.float32)
    rows_per_block = NC // col_count
    chunk = pair_count // PAIR_CHUNKS
    starts = list(range(0, pair_count, chunk))

    def cond_block(first, delta):
        cond_a = conduction[first : first + chunk]
        cond_b = conduction[pair_count + first : pair_count + first + chunk]
        rows = lax.dynamic_slice_in_dim(
            cond_a, (col_index ^ delta) * rows_per_block, rows_per_block, 1
        )
        cond_pairs = (rows[:, :, None, :] * cond_b[:, None, :, :]).astype(jnp.bfloat16)
        return cond_pairs.reshape(chunk, rows_per_block * NC, mu_cols)

    cond_blocks = [[cond_block(first, d) for d in range(col_count)] for first in starts]

    valence, cond_blocks = gather_axis(
        jnp.take(held_valence, wanted, axis=0), "col", tie=cond_blocks
    )

    def valence_of(first):
        return (
            valence[:, first : first + chunk],
            valence[:, pair_count + first : pair_count + first + chunk],
        )

    results = []
    screened = screened_of(*valence_of(starts[0]), screening[0])
    for n_chunk, first in enumerate(starts):

        def own_block(delta, screened=screened, blocks=cond_blocks[n_chunk]):
            cond_pairs = blocks[delta]
            return jnp.einsum(
                "pan,pbn->pab", screened, cond_pairs, preferred_element_type=jnp.float32
            )

        def last_swap(send, bit):
            got = swap(send.astype(jnp.bfloat16), "col", bit)
            return got.astype(jnp.float32), None

        summed, _ = scatter_sum_col(own_block, last_swap)
        results.append(summed)
        if n_chunk + 1 < len(starts):
            screened = screened_of(*valence_of(starts[n_chunk + 1]), screening[0])
    return jnp.concatenate(results, 0)[None]


def solution(mesh):
    placed = (P("pb", None, "col"), P("pb", None, "col"), P("pb", None))
    return jax.shard_map(
        body, mesh=mesh, in_specs=placed, out_specs=P("pb", None, None, "col"), check_vma=False
    )
```

```python
import jax
import jax.numpy as jnp
from jax import lax
from jax.sharding import PartitionSpec as P

NV = 16
NC = 32
PAIR_CHUNKS = 2


def swap(x, axis, bit):
    size = lax.axis_size(axis)
    return lax.ppermute(x, axis, [(i, i ^ bit) for i in range(size)])


def gather_axis(mine, axis):
    count = lax.axis_size(axis)
    me = lax.axis_index(axis)
    cur = mine[None]
    bit = count // 2
    while bit >= 1:
        got = swap(cur, axis, bit)
        low = (me & bit) == 0
        cur = jnp.where(low, jnp.stack([cur, got], 1), jnp.stack([got, cur], 1))
        cur = cur.reshape((-1,) + mine.shape)
        bit //= 2
    return cur


def scatter_sum_col(own_block, last_swap):
    col_count = lax.axis_size("col")
    acc = {}
    extra = None
    bit = 1
    while bit < col_count:
        deltas = [d for d in range(col_count) if d & bit and d % bit == 0]
        send = []
        for d in deltas:
            value = acc.pop(d) if d in acc else own_block(d)
            send.append(value)
        send = jnp.stack(send)
        if bit * 2 >= col_count:
            got, extra = last_swap(send, bit)
        else:
            got = swap(send, "col", bit)
        for i, d in enumerate(deltas):
            kept = d ^ bit
            base = acc.pop(kept) if kept in acc else own_block(kept)
            acc[kept] = base + got[i]
        bit *= 2
    return (acc[0] if 0 in acc else own_block(0)), extra


def screened_of(valence_a, valence_b, screening):
    col_count, chunk, _, mu_cols = valence_a.shape
    valence_a = valence_a.astype(jnp.float32)
    valence_b = valence_b.astype(jnp.float32)
    val_pairs = (valence_a[:, :, :, None, :] * valence_b[:, :, None, :, :]).astype(jnp.bfloat16)
    val_pairs = val_pairs.reshape(col_count, chunk * NV * NV, mu_cols)
    screen = screening.reshape(col_count, mu_cols, screening.shape[1])
    screened = lax.dot_general(
        val_pairs, screen, (((0, 2), (0, 1)), ((), ())), preferred_element_type=jnp.float32
    ).astype(jnp.bfloat16)
    return screened.reshape(chunk, NV * NV, screening.shape[1])


def body(orbitals, screening, pairs_k):
    k_dev, orb_count, mu_cols = orbitals.shape
    group_count = lax.axis_size("pb")
    col_count = lax.axis_size("col")
    kpoint_count = k_dev * group_count
    group_index = lax.axis_index("pb")
    col_index = lax.axis_index("col")
    kpoint_a = pairs_k[0]
    kpoint_b = (kpoint_a - group_index) % kpoint_count
    pair_count = kpoint_a.shape[0]

    wanted = jnp.concatenate([kpoint_a, kpoint_b])
    held_valence = gather_axis(orbitals[:, :NV, :], "pb").reshape(kpoint_count, NV, mu_cols)
    chosen_valence = jnp.take(held_valence, wanted, axis=0)
    conduction_mine, chosen_valence = lax.optimization_barrier(
        (orbitals[:, NV:, :], chosen_valence)
    )
    held_conduction = gather_axis(conduction_mine, "pb").reshape(
        kpoint_count, orb_count - NV, mu_cols
    )

    valence = gather_axis(chosen_valence, "col")
    conduction = jnp.take(held_conduction, wanted, axis=0).astype(jnp.float32)
    rows_per_block = NC // col_count
    chunk = pair_count // PAIR_CHUNKS
    starts = list(range(0, pair_count, chunk))

    def valence_of(first):
        return (
            valence[:, first : first + chunk],
            valence[:, pair_count + first : pair_count + first + chunk],
        )

    results = []
    screened = screened_of(*valence_of(starts[0]), screening[0])
    for n_chunk, first in enumerate(starts):
        cond_a = conduction[first : first + chunk]
        cond_b = conduction[pair_count + first : pair_count + first + chunk]

        def own_block(delta, screened=screened, cond_a=cond_a, cond_b=cond_b):
            block = col_index ^ delta
            rows = lax.dynamic_slice_in_dim(cond_a, block * rows_per_block, rows_per_block, 1)
            cond_pairs = (rows[:, :, None, :] * cond_b[:, None, :, :]).astype(jnp.bfloat16)
            cond_pairs = cond_pairs.reshape(chunk, rows_per_block * NC, mu_cols)
            return jnp.einsum(
                "pan,pbn->pab", screened, cond_pairs, preferred_element_type=jnp.float32
            )

        def last_swap(send, bit):
            got = swap(send.astype(jnp.bfloat16), "col", bit)
            return got.astype(jnp.float32), None

        summed, _ = scatter_sum_col(own_block, last_swap)
        results.append(summed)
        if n_chunk + 1 < len(starts):
            screened = screened_of(*valence_of(starts[n_chunk + 1]), screening[0])
    return jnp.concatenate(results, 0)[None]


def solution(mesh):
    placed = (P("pb", None, "col"), P("pb", None, "col"), P("pb", None))
    return jax.shard_map(
        body, mesh=mesh, in_specs=placed, out_specs=P("pb", None, None, "col"), check_vma=False
    )
```

```python
import jax
import jax.numpy as jnp
from jax import lax
from jax.sharding import PartitionSpec as P

NV = 16
NC = 32
PAIR_CHUNKS = 2


def swap(x, axis, bit):
    size = lax.axis_size(axis)
    return lax.ppermute(x, axis, [(i, i ^ bit) for i in range(size)])


def gather_axis(mine, axis):
    count = lax.axis_size(axis)
    me = lax.axis_index(axis)
    cur = mine[None]
    bit = count // 2
    while bit >= 1:
        got = swap(cur, axis, bit)
        low = (me & bit) == 0
        cur = jnp.where(low, jnp.stack([cur, got], 1), jnp.stack([got, cur], 1))
        cur = cur.reshape((-1,) + mine.shape)
        bit //= 2
    return cur


def scatter_sum_col(own_block, last_swap):
    col_count = lax.axis_size("col")
    acc = {}
    extra = None
    bit = 1
    while bit < col_count:
        deltas = [d for d in range(col_count) if d & bit and d % bit == 0]
        send = []
        for d in deltas:
            value = acc.pop(d) if d in acc else own_block(d)
            send.append(value)
        send = jnp.stack(send)
        if bit * 2 >= col_count:
            got, extra = last_swap(send, bit)
        else:
            got = swap(send, "col", bit)
        for i, d in enumerate(deltas):
            kept = d ^ bit
            base = acc.pop(kept) if kept in acc else own_block(kept)
            acc[kept] = base + got[i]
        bit *= 2
    return (acc[0] if 0 in acc else own_block(0)), extra


def screened_of(valence_a, valence_b, screening):
    col_count, chunk, _, mu_cols = valence_a.shape
    valence_a = valence_a.astype(jnp.float32)
    valence_b = valence_b.astype(jnp.float32)
    val_pairs = (valence_a[:, :, :, None, :] * valence_b[:, :, None, :, :]).astype(jnp.bfloat16)
    val_pairs = val_pairs.reshape(col_count, chunk * NV * NV, mu_cols)
    screen = screening.reshape(col_count, mu_cols, screening.shape[1])
    screened = lax.dot_general(
        val_pairs, screen, (((0, 2), (0, 1)), ((), ())), preferred_element_type=jnp.float32
    ).astype(jnp.bfloat16)
    return screened.reshape(chunk, NV * NV, screening.shape[1])


def body(orbitals, screening, pairs_k):
    k_dev, orb_count, mu_cols = orbitals.shape
    group_count = lax.axis_size("pb")
    col_count = lax.axis_size("col")
    kpoint_count = k_dev * group_count
    group_index = lax.axis_index("pb")
    col_index = lax.axis_index("col")
    kpoint_a = pairs_k[0]
    kpoint_b = (kpoint_a - group_index) % kpoint_count
    pair_count = kpoint_a.shape[0]

    wanted = jnp.concatenate([kpoint_a, kpoint_b])
    held_valence = gather_axis(orbitals[:, :NV, :], "pb").reshape(kpoint_count, NV, mu_cols)
    held_conduction = gather_axis(orbitals[:, NV:, :], "pb").reshape(
        kpoint_count, orb_count - NV, mu_cols
    )

    valence = gather_axis(jnp.take(held_valence, wanted, axis=0), "col")
    conduction = jnp.take(held_conduction, wanted, axis=0).astype(jnp.float32)
    rows_per_block = NC // col_count
    chunk = pair_count // PAIR_CHUNKS
    starts = list(range(0, pair_count, chunk))

    def cond_block(first, delta):
        cond_a = conduction[first : first + chunk]
        cond_b = conduction[pair_count + first : pair_count + first + chunk]
        rows = lax.dynamic_slice_in_dim(
            cond_a, (col_index ^ delta) * rows_per_block, rows_per_block, 1
        )
        cond_pairs = (rows[:, :, None, :] * cond_b[:, None, :, :]).astype(jnp.bfloat16)
        return cond_pairs.reshape(chunk, rows_per_block * NC, mu_cols)

    cond_blocks = [[cond_block(first, d) for d in range(col_count)] for first in starts]
    valence, cond_blocks = lax.optimization_barrier((valence, cond_blocks))

    def valence_of(first):
        return (
            valence[:, first : first + chunk],
            valence[:, pair_count + first : pair_count + first + chunk],
        )

    results = []
    screened = screened_of(*valence_of(starts[0]), screening[0])
    for n_chunk, first in enumerate(starts):

        def own_block(delta, screened=screened, blocks=cond_blocks[n_chunk]):
            cond_pairs = blocks[delta]
            return jnp.einsum(
                "pan,pbn->pab", screened, cond_pairs, preferred_element_type=jnp.float32
            )

        def last_swap(send, bit):
            got = swap(send.astype(jnp.bfloat16), "col", bit)
            return got.astype(jnp.float32), None

        summed, _ = scatter_sum_col(own_block, last_swap)
        results.append(summed)
        if n_chunk + 1 < len(starts):
            screened = screened_of(*valence_of(starts[n_chunk + 1]), screening[0])
    return jnp.concatenate(results, 0)[None]


def solution(mesh):
    placed = (P("pb", None, "col"), P("pb", None, "col"), P("pb", None))
    return jax.shard_map(
        body, mesh=mesh, in_specs=placed, out_specs=P("pb", None, None, "col"), check_vma=False
    )
```

```python
import jax
import jax.numpy as jnp
from jax import lax
from jax.sharding import PartitionSpec as P

NV = 16
NC = 32
PAIR_CHUNKS = 2


def swap(x, axis, bit):
    size = lax.axis_size(axis)
    return lax.ppermute(x, axis, [(i, i ^ bit) for i in range(size)])


def gather_axis(mine, axis, tie=None):
    count = lax.axis_size(axis)
    me = lax.axis_index(axis)
    cur = mine[None]
    bit = count // 2
    while bit >= 1:
        got = swap(cur, axis, bit)
        low = (me & bit) == 0
        cur = jnp.where(low, jnp.stack([cur, got], 1), jnp.stack([got, cur], 1))
        cur = cur.reshape((-1,) + mine.shape)
        if tie is not None and bit > 1:
            cur, tie = lax.optimization_barrier((cur, tie))
        bit //= 2
    if tie is None:
        return cur
    return cur, tie


def scatter_sum_col(own_block, last_swap):
    col_count = lax.axis_size("col")
    acc = {}
    extra = None
    bit = 1
    while bit < col_count:
        deltas = [d for d in range(col_count) if d & bit and d % bit == 0]
        send = []
        for d in deltas:
            value = acc.pop(d) if d in acc else own_block(d)
            send.append(value)
        send = jnp.stack(send)
        if bit * 2 >= col_count:
            got, extra = last_swap(send, bit)
        else:
            got = swap(send, "col", bit)
        for i, d in enumerate(deltas):
            kept = d ^ bit
            base = acc.pop(kept) if kept in acc else own_block(kept)
            acc[kept] = base + got[i]
        bit *= 2
    return (acc[0] if 0 in acc else own_block(0)), extra


def screened_of(valence_a, valence_b, screening):
    col_count, chunk, _, mu_cols = valence_a.shape
    valence_a = valence_a.astype(jnp.float32)
    valence_b = valence_b.astype(jnp.float32)
    val_pairs = (valence_a[:, :, :, None, :] * valence_b[:, :, None, :, :]).astype(jnp.bfloat16)
    val_pairs = val_pairs.reshape(col_count, chunk * NV * NV, mu_cols)
    screen = screening.reshape(col_count, mu_cols, screening.shape[1])
    screened = lax.dot_general(
        val_pairs, screen, (((0, 2), (0, 1)), ((), ())), preferred_element_type=jnp.float32
    ).astype(jnp.bfloat16)
    return screened.reshape(chunk, NV * NV, screening.shape[1])


def body(orbitals, screening, pairs_k):
    k_dev, orb_count, mu_cols = orbitals.shape
    group_count = lax.axis_size("pb")
    col_count = lax.axis_size("col")
    kpoint_count = k_dev * group_count
    group_index = lax.axis_index("pb")
    col_index = lax.axis_index("col")
    kpoint_a = pairs_k[0]
    kpoint_b = (kpoint_a - group_index) % kpoint_count
    pair_count = kpoint_a.shape[0]

    wanted = jnp.concatenate([kpoint_a, kpoint_b])
    held_valence = gather_axis(orbitals[:, :NV, :], "pb").reshape(kpoint_count, NV, mu_cols)
    held_conduction = gather_axis(orbitals[:, NV:, :], "pb").reshape(
        kpoint_count, orb_count - NV, mu_cols
    )

    conduction = jnp.take(held_conduction, wanted, axis=0).astype(jnp.float32)
    rows_per_block = NC // col_count
    chunk = pair_count // PAIR_CHUNKS
    starts = list(range(0, pair_count, chunk))

    def cond_block(first, delta):
        cond_a = conduction[first : first + chunk]
        cond_b = conduction[pair_count + first : pair_count + first + chunk]
        rows = lax.dynamic_slice_in_dim(
            cond_a, (col_index ^ delta) * rows_per_block, rows_per_block, 1
        )
        cond_pairs = (rows[:, :, None, :] * cond_b[:, None, :, :]).astype(jnp.bfloat16)
        return cond_pairs.reshape(chunk, rows_per_block * NC, mu_cols)

    cond_blocks = [[cond_block(first, d) for d in range(col_count)] for first in starts]
    valence, cond_blocks = gather_axis(
        jnp.take(held_valence, wanted, axis=0), "col", tie=cond_blocks
    )

    def valence_of(first):
        return (
            valence[:, first : first + chunk],
            valence[:, pair_count + first : pair_count + first + chunk],
        )

    results = []
    screened = screened_of(*valence_of(starts[0]), screening[0])
    for n_chunk, first in enumerate(starts):

        def own_block(delta, screened=screened, blocks=cond_blocks[n_chunk]):
            cond_pairs = blocks[delta]
            return jnp.einsum(
                "pan,pbn->pab", screened, cond_pairs, preferred_element_type=jnp.float32
            )

        def last_swap(send, bit):
            got = swap(send.astype(jnp.bfloat16), "col", bit)
            return got.astype(jnp.float32), None

        summed, _ = scatter_sum_col(own_block, last_swap)
        results.append(summed)
        if n_chunk + 1 < len(starts):
            screened = screened_of(*valence_of(starts[n_chunk + 1]), screening[0])
    return jnp.concatenate(results, 0)[None]


def solution(mesh):
    placed = (P("pb", None, "col"), P("pb", None, "col"), P("pb", None))
    return jax.shard_map(
        body, mesh=mesh, in_specs=placed, out_specs=P("pb", None, None, "col"), check_vma=False
    )
```

```python
import jax
import jax.numpy as jnp
from jax import lax
from jax.sharding import PartitionSpec as P

NV = 16
NC = 32


def swap(x, axis, bit):
    size = lax.axis_size(axis)
    return lax.ppermute(x, axis, [(i, i ^ bit) for i in range(size)])


def gather_axis(mine, axis):
    count = lax.axis_size(axis)
    me = lax.axis_index(axis)
    cur = mine[None]
    bit = count // 2
    while bit >= 1:
        got = swap(cur, axis, bit)
        low = (me & bit) == 0
        cur = jnp.where(low, jnp.stack([cur, got], 1), jnp.stack([got, cur], 1))
        cur = cur.reshape((-1,) + mine.shape)
        bit //= 2
    return cur


def scatter_sum_col(own_block, last_swap):
    col_count = lax.axis_size("col")
    acc = {}
    extra = None
    bit = 1
    while bit < col_count:
        deltas = [d for d in range(col_count) if d & bit and d % bit == 0]
        send = []
        for d in deltas:
            value = acc.pop(d) if d in acc else own_block(d)
            send.append(value)
        send = jnp.stack(send)
        if bit * 2 >= col_count:
            got, extra = last_swap(send, bit)
        else:
            got = swap(send, "col", bit)
        for i, d in enumerate(deltas):
            kept = d ^ bit
            base = acc.pop(kept) if kept in acc else own_block(kept)
            acc[kept] = base + got[i]
        bit *= 2
    return (acc[0] if 0 in acc else own_block(0)), extra


def screened_of(valence_a, valence_b, screening):
    col_count, chunk, _, mu_cols = valence_a.shape
    valence_a = valence_a.astype(jnp.float32)
    valence_b = valence_b.astype(jnp.float32)
    val_pairs = (valence_a[:, :, :, None, :] * valence_b[:, :, None, :, :]).astype(jnp.bfloat16)
    val_pairs = val_pairs.reshape(col_count, chunk * NV * NV, mu_cols)
    screen = screening.reshape(col_count, mu_cols, screening.shape[1])
    screened = lax.dot_general(
        val_pairs, screen, (((0, 2), (0, 1)), ((), ())), preferred_element_type=jnp.float32
    ).astype(jnp.bfloat16)
    return screened.reshape(chunk, NV * NV, screening.shape[1])


def body(orbitals, screening, pairs_k):
    k_dev, orb_count, mu_cols = orbitals.shape
    group_count = lax.axis_size("pb")
    col_count = lax.axis_size("col")
    kpoint_count = k_dev * group_count
    group_index = lax.axis_index("pb")
    col_index = lax.axis_index("col")
    kpoint_a = pairs_k[0]
    kpoint_b = (kpoint_a - group_index) % kpoint_count
    pair_count = kpoint_a.shape[0]

    wanted = jnp.concatenate([kpoint_a, kpoint_b])
    held_valence = gather_axis(orbitals[:, :NV, :], "pb").reshape(kpoint_count, NV, mu_cols)
    held_conduction = gather_axis(orbitals[:, NV:, :], "pb").reshape(
        kpoint_count, orb_count - NV, mu_cols
    )

    valence = gather_axis(jnp.take(held_valence, wanted, axis=0), "col")
    conduction = jnp.take(held_conduction, wanted, axis=0).astype(jnp.float32)
    rows_per_block = NC // col_count
    first_size = max(1, pair_count // 4)
    bounds = [(0, first_size), (first_size, pair_count - first_size)]

    def cond_block(first, chunk, delta):
        cond_a = conduction[first : first + chunk]
        cond_b = conduction[pair_count + first : pair_count + first + chunk]
        rows = lax.dynamic_slice_in_dim(
            cond_a, (col_index ^ delta) * rows_per_block, rows_per_block, 1
        )
        cond_pairs = (rows[:, :, None, :] * cond_b[:, None, :, :]).astype(jnp.bfloat16)
        return cond_pairs.reshape(chunk, rows_per_block * NC, mu_cols)

    cond_blocks = [[cond_block(first, size, d) for d in range(col_count)] for first, size in bounds]
    valence, cond_blocks = lax.optimization_barrier((valence, cond_blocks))

    def valence_of(first, chunk):
        return (
            valence[:, first : first + chunk],
            valence[:, pair_count + first : pair_count + first + chunk],
        )

    results = []
    screened = screened_of(*valence_of(*bounds[0]), screening[0])
    for n_chunk, (first, chunk) in enumerate(bounds):

        def own_block(delta, screened=screened, blocks=cond_blocks[n_chunk], chunk=chunk):
            cond_pairs = blocks[delta]
            return jnp.einsum(
                "pan,pbn->pab", screened, cond_pairs, preferred_element_type=jnp.float32
            )

        following = valence_of(*bounds[n_chunk + 1]) if n_chunk + 1 < len(bounds) else None

        def last_swap(send, bit, following=following):
            send = send.astype(jnp.bfloat16)
            if following is None:
                return swap(send, "col", bit).astype(jnp.float32), None
            send, following = lax.optimization_barrier((send, following))
            got = swap(send, "col", bit)
            screened_next = screened_of(*following, screening[0])
            got, screened_next = lax.optimization_barrier((got, screened_next))
            return got.astype(jnp.float32), screened_next

        summed, screened = scatter_sum_col(own_block, last_swap)
        results.append(summed)
    return jnp.concatenate(results, 0)[None]


def solution(mesh):
    placed = (P("pb", None, "col"), P("pb", None, "col"), P("pb", None))
    return jax.shard_map(
        body, mesh=mesh, in_specs=placed, out_specs=P("pb", None, None, "col"), check_vma=False
    )
```

```python
import jax
import jax.numpy as jnp
from jax import lax
from jax.sharding import PartitionSpec as P

NV = 16
NC = 32
PAIR_CHUNKS = 4


def swap(x, axis, bit):
    size = lax.axis_size(axis)
    return lax.ppermute(x, axis, [(i, i ^ bit) for i in range(size)])


def gather_axis(mine, axis):
    count = lax.axis_size(axis)
    me = lax.axis_index(axis)
    cur = mine[None]
    bit = count // 2
    while bit >= 1:
        got = swap(cur, axis, bit)
        low = (me & bit) == 0
        cur = jnp.where(low, jnp.stack([cur, got], 1), jnp.stack([got, cur], 1))
        cur = cur.reshape((-1,) + mine.shape)
        bit //= 2
    return cur


def scatter_sum_col(own_block, last_swap):
    col_count = lax.axis_size("col")
    acc = {}
    extra = None
    bit = 1
    while bit < col_count:
        deltas = [d for d in range(col_count) if d & bit and d % bit == 0]
        send = []
        for d in deltas:
            value = acc.pop(d) if d in acc else own_block(d)
            send.append(value)
        send = jnp.stack(send)
        if bit * 2 >= col_count:
            got, extra = last_swap(send, bit)
        else:
            got = swap(send, "col", bit)
        for i, d in enumerate(deltas):
            kept = d ^ bit
            base = acc.pop(kept) if kept in acc else own_block(kept)
            acc[kept] = base + got[i]
        bit *= 2
    return (acc[0] if 0 in acc else own_block(0)), extra


def screened_of(valence_a, valence_b, screening):
    col_count, chunk, _, mu_cols = valence_a.shape
    valence_a = valence_a.astype(jnp.float32)
    valence_b = valence_b.astype(jnp.float32)
    val_pairs = (valence_a[:, :, :, None, :] * valence_b[:, :, None, :, :]).astype(jnp.bfloat16)
    val_pairs = val_pairs.reshape(col_count, chunk * NV * NV, mu_cols)
    screen = screening.reshape(col_count, mu_cols, screening.shape[1])
    screened = lax.dot_general(
        val_pairs, screen, (((0, 2), (0, 1)), ((), ())), preferred_element_type=jnp.float32
    ).astype(jnp.bfloat16)
    return screened.reshape(chunk, NV * NV, screening.shape[1])


def body(orbitals, screening, pairs_k):
    k_dev, orb_count, mu_cols = orbitals.shape
    group_count = lax.axis_size("pb")
    col_count = lax.axis_size("col")
    kpoint_count = k_dev * group_count
    group_index = lax.axis_index("pb")
    col_index = lax.axis_index("col")
    kpoint_a = pairs_k[0]
    kpoint_b = (kpoint_a - group_index) % kpoint_count
    pair_count = kpoint_a.shape[0]

    wanted = jnp.concatenate([kpoint_a, kpoint_b])
    held_valence = gather_axis(orbitals[:, :NV, :], "pb").reshape(kpoint_count, NV, mu_cols)
    held_conduction = gather_axis(orbitals[:, NV:, :], "pb").reshape(
        kpoint_count, orb_count - NV, mu_cols
    )

    valence = gather_axis(jnp.take(held_valence, wanted, axis=0), "col")
    conduction = jnp.take(held_conduction, wanted, axis=0).astype(jnp.float32)
    rows_per_block = NC // col_count
    chunk = pair_count // PAIR_CHUNKS
    starts = list(range(0, pair_count, chunk))

    def cond_block(first, delta):
        cond_a = conduction[first : first + chunk]
        cond_b = conduction[pair_count + first : pair_count + first + chunk]
        rows = lax.dynamic_slice_in_dim(
            cond_a, (col_index ^ delta) * rows_per_block, rows_per_block, 1
        )
        cond_pairs = (rows[:, :, None, :] * cond_b[:, None, :, :]).astype(jnp.bfloat16)
        return cond_pairs.reshape(chunk, rows_per_block * NC, mu_cols)

    cond_blocks = [[cond_block(first, d) for d in range(col_count)] for first in starts]
    valence, cond_blocks = lax.optimization_barrier((valence, cond_blocks))

    def valence_of(first):
        return (
            valence[:, first : first + chunk],
            valence[:, pair_count + first : pair_count + first + chunk],
        )

    results = []
    screened = screened_of(*valence_of(starts[0]), screening[0])
    for n_chunk, first in enumerate(starts):

        def own_block(delta, screened=screened, blocks=cond_blocks[n_chunk]):
            cond_pairs = blocks[delta]
            return jnp.einsum(
                "pan,pbn->pab", screened, cond_pairs, preferred_element_type=jnp.float32
            )

        def last_swap(send, bit):
            got = swap(send.astype(jnp.bfloat16), "col", bit)
            return got.astype(jnp.float32), None

        summed, _ = scatter_sum_col(own_block, last_swap)
        results.append(summed)
        if n_chunk + 1 < len(starts):
            screened = screened_of(*valence_of(starts[n_chunk + 1]), screening[0])
    return jnp.concatenate(results, 0)[None]


def solution(mesh):
    placed = (P("pb", None, "col"), P("pb", None, "col"), P("pb", None))
    return jax.shard_map(
        body, mesh=mesh, in_specs=placed, out_specs=P("pb", None, None, "col"), check_vma=False
    )
```

```python
import jax
import jax.numpy as jnp
from jax import lax
from jax.sharding import PartitionSpec as P

NV = 16
NC = 32
PAIR_CHUNKS = 2


def gather_axis_low_first(mine, axis):
    count = lax.axis_size(axis)
    me = lax.axis_index(axis)
    cur = mine[None]
    bit = 1
    while bit < count:
        got = swap(cur, axis, bit)
        low = (me & bit) == 0
        cur = jnp.where(low, jnp.concatenate([cur, got], 0), jnp.concatenate([got, cur], 0))
        bit *= 2
    return cur


def swap(x, axis, bit):
    size = lax.axis_size(axis)
    return lax.ppermute(x, axis, [(i, i ^ bit) for i in range(size)])


def gather_axis(mine, axis):
    count = lax.axis_size(axis)
    me = lax.axis_index(axis)
    cur = mine[None]
    bit = count // 2
    while bit >= 1:
        got = swap(cur, axis, bit)
        low = (me & bit) == 0
        cur = jnp.where(low, jnp.stack([cur, got], 1), jnp.stack([got, cur], 1))
        cur = cur.reshape((-1,) + mine.shape)
        bit //= 2
    return cur


def scatter_sum_col(own_block, last_swap):
    col_count = lax.axis_size("col")
    acc = {}
    extra = None
    bit = 1
    while bit < col_count:
        deltas = [d for d in range(col_count) if d & bit and d % bit == 0]
        send = []
        for d in deltas:
            value = acc.pop(d) if d in acc else own_block(d)
            send.append(value)
        send = jnp.stack(send)
        if bit * 2 >= col_count:
            got, extra = last_swap(send, bit)
        else:
            got = swap(send, "col", bit)
        for i, d in enumerate(deltas):
            kept = d ^ bit
            base = acc.pop(kept) if kept in acc else own_block(kept)
            acc[kept] = base + got[i]
        bit *= 2
    return (acc[0] if 0 in acc else own_block(0)), extra


def screened_of(valence_a, valence_b, screening):
    col_count, chunk, _, mu_cols = valence_a.shape
    valence_a = valence_a.astype(jnp.float32)
    valence_b = valence_b.astype(jnp.float32)
    val_pairs = (valence_a[:, :, :, None, :] * valence_b[:, :, None, :, :]).astype(jnp.bfloat16)
    val_pairs = val_pairs.reshape(col_count, chunk * NV * NV, mu_cols)
    screen = screening.reshape(col_count, mu_cols, screening.shape[1])
    screened = lax.dot_general(
        val_pairs, screen, (((0, 2), (0, 1)), ((), ())), preferred_element_type=jnp.float32
    ).astype(jnp.bfloat16)
    return screened.reshape(chunk, NV * NV, screening.shape[1])


def body(orbitals, screening, pairs_k):
    k_dev, orb_count, mu_cols = orbitals.shape
    group_count = lax.axis_size("pb")
    col_count = lax.axis_size("col")
    kpoint_count = k_dev * group_count
    group_index = lax.axis_index("pb")
    col_index = lax.axis_index("col")
    kpoint_a = pairs_k[0]
    kpoint_b = (kpoint_a - group_index) % kpoint_count
    pair_count = kpoint_a.shape[0]

    wanted = jnp.concatenate([kpoint_a, kpoint_b])
    held_valence = gather_axis(orbitals[:, :NV, :], "pb").reshape(kpoint_count, NV, mu_cols)
    held_conduction = gather_axis_low_first(orbitals[:, NV:, :], "pb").reshape(
        kpoint_count, orb_count - NV, mu_cols
    )

    valence = gather_axis(jnp.take(held_valence, wanted, axis=0), "col")
    conduction = jnp.take(held_conduction, wanted, axis=0).astype(jnp.float32)
    rows_per_block = NC // col_count
    chunk = pair_count // PAIR_CHUNKS
    starts = list(range(0, pair_count, chunk))

    def cond_block(first, delta):
        cond_a = conduction[first : first + chunk]
        cond_b = conduction[pair_count + first : pair_count + first + chunk]
        rows = lax.dynamic_slice_in_dim(
            cond_a, (col_index ^ delta) * rows_per_block, rows_per_block, 1
        )
        cond_pairs = (rows[:, :, None, :] * cond_b[:, None, :, :]).astype(jnp.bfloat16)
        return cond_pairs.reshape(chunk, rows_per_block * NC, mu_cols)

    cond_blocks = [[cond_block(first, d) for d in range(col_count)] for first in starts]
    valence, cond_blocks = lax.optimization_barrier((valence, cond_blocks))

    def valence_of(first):
        return (
            valence[:, first : first + chunk],
            valence[:, pair_count + first : pair_count + first + chunk],
        )

    results = []
    screened = screened_of(*valence_of(starts[0]), screening[0])
    for n_chunk, first in enumerate(starts):

        def own_block(delta, screened=screened, blocks=cond_blocks[n_chunk]):
            cond_pairs = blocks[delta]
            return jnp.einsum(
                "pan,pbn->pab", screened, cond_pairs, preferred_element_type=jnp.float32
            )

        def last_swap(send, bit):
            got = swap(send.astype(jnp.bfloat16), "col", bit)
            return got.astype(jnp.float32), None

        summed, _ = scatter_sum_col(own_block, last_swap)
        results.append(summed)
        if n_chunk + 1 < len(starts):
            screened = screened_of(*valence_of(starts[n_chunk + 1]), screening[0])
    return jnp.concatenate(results, 0)[None]


def solution(mesh):
    placed = (P("pb", None, "col"), P("pb", None, "col"), P("pb", None))
    return jax.shard_map(
        body, mesh=mesh, in_specs=placed, out_specs=P("pb", None, None, "col"), check_vma=False
    )
```

```python
import jax
import jax.numpy as jnp
from jax import lax
from jax.sharding import PartitionSpec as P

NV = 16
NC = 32
PAIR_CHUNKS = 2


def swap(x, axis, bit):
    size = lax.axis_size(axis)
    return lax.ppermute(x, axis, [(i, i ^ bit) for i in range(size)])


def gather_axis(mine, axis):
    count = lax.axis_size(axis)
    me = lax.axis_index(axis)
    cur = mine[None]
    bit = count // 2
    while bit >= 1:
        got = swap(cur, axis, bit)
        low = (me & bit) == 0
        cur = jnp.where(low, jnp.stack([cur, got], 1), jnp.stack([got, cur], 1))
        cur = cur.reshape((-1,) + mine.shape)
        bit //= 2
    return cur


def scatter_sum_col(own_block, last_swap):
    col_count = lax.axis_size("col")
    acc = {}
    extra = None
    bit = 1
    while bit < col_count:
        deltas = [d for d in range(col_count) if d & bit and d % bit == 0]
        send = []
        for d in deltas:
            value = acc.pop(d) if d in acc else own_block(d)
            send.append(value)
        send = jnp.stack(send)
        if bit * 2 >= col_count:
            got, extra = last_swap(send, bit)
        else:
            got = swap(send, "col", bit)
        for i, d in enumerate(deltas):
            kept = d ^ bit
            base = acc.pop(kept) if kept in acc else own_block(kept)
            acc[kept] = base + got[i]
        bit *= 2
    return (acc[0] if 0 in acc else own_block(0)), extra


def pairs_of(valence_a, valence_b):
    col_count, chunk, _, mu_cols = valence_a.shape
    valence_a = valence_a.astype(jnp.float32)
    valence_b = valence_b.astype(jnp.float32)
    val_pairs = (valence_a[:, :, :, None, :] * valence_b[:, :, None, :, :]).astype(jnp.bfloat16)
    return val_pairs.reshape(col_count, chunk * NV * NV, mu_cols)


def screened_of(valence_a, valence_b, screening):
    return dot_of(pairs_of(valence_a, valence_b), screening)


def dot_of(val_pairs, screening):
    col_count, rows, mu_cols = val_pairs.shape
    chunk = rows // (NV * NV)
    screen = screening.reshape(col_count, mu_cols, screening.shape[1])
    screened = lax.dot_general(
        val_pairs, screen, (((0, 2), (0, 1)), ((), ())), preferred_element_type=jnp.float32
    ).astype(jnp.bfloat16)
    return screened.reshape(chunk, NV * NV, screening.shape[1])


def body(orbitals, screening, pairs_k):
    k_dev, orb_count, mu_cols = orbitals.shape
    group_count = lax.axis_size("pb")
    col_count = lax.axis_size("col")
    kpoint_count = k_dev * group_count
    group_index = lax.axis_index("pb")
    col_index = lax.axis_index("col")
    kpoint_a = pairs_k[0]
    kpoint_b = (kpoint_a - group_index) % kpoint_count
    pair_count = kpoint_a.shape[0]

    wanted = jnp.concatenate([kpoint_a, kpoint_b])
    held_valence = gather_axis(orbitals[:, :NV, :], "pb").reshape(kpoint_count, NV, mu_cols)
    held_conduction = gather_axis(orbitals[:, NV:, :], "pb").reshape(
        kpoint_count, orb_count - NV, mu_cols
    )

    valence = gather_axis(jnp.take(held_valence, wanted, axis=0), "col")
    conduction = jnp.take(held_conduction, wanted, axis=0).astype(jnp.float32)
    rows_per_block = NC // col_count
    chunk = pair_count // PAIR_CHUNKS
    starts = list(range(0, pair_count, chunk))

    def cond_block(first, delta):
        cond_a = conduction[first : first + chunk]
        cond_b = conduction[pair_count + first : pair_count + first + chunk]
        rows = lax.dynamic_slice_in_dim(
            cond_a, (col_index ^ delta) * rows_per_block, rows_per_block, 1
        )
        cond_pairs = (rows[:, :, None, :] * cond_b[:, None, :, :]).astype(jnp.bfloat16)
        return cond_pairs.reshape(chunk, rows_per_block * NC, mu_cols)

    cond_blocks = [[cond_block(first, d) for d in range(col_count)] for first in starts]
    valence, cond_blocks = lax.optimization_barrier((valence, cond_blocks))

    def valence_of(first):
        return (
            valence[:, first : first + chunk],
            valence[:, pair_count + first : pair_count + first + chunk],
        )

    results = []
    screened = screened_of(*valence_of(starts[0]), screening[0])
    for n_chunk, first in enumerate(starts):

        def own_block(delta, screened=screened, blocks=cond_blocks[n_chunk]):
            cond_pairs = blocks[delta]
            return jnp.einsum(
                "pan,pbn->pab", screened, cond_pairs, preferred_element_type=jnp.float32
            )

        following = valence_of(starts[n_chunk + 1]) if n_chunk + 1 < len(starts) else None

        def last_swap(send, bit, following=following):
            send = send.astype(jnp.bfloat16)
            if following is None:
                return swap(send, "col", bit).astype(jnp.float32), None
            val_next = pairs_of(*following)
            send, val_next = lax.optimization_barrier((send, val_next))
            got = swap(send, "col", bit)
            screened_next = dot_of(val_next, screening[0])
            got, screened_next = lax.optimization_barrier((got, screened_next))
            return got.astype(jnp.float32), screened_next

        summed, screened = scatter_sum_col(own_block, last_swap)
        results.append(summed)
    return jnp.concatenate(results, 0)[None]


def solution(mesh):
    placed = (P("pb", None, "col"), P("pb", None, "col"), P("pb", None))
    return jax.shard_map(
        body, mesh=mesh, in_specs=placed, out_specs=P("pb", None, None, "col"), check_vma=False
    )
```

```python
import jax
import jax.numpy as jnp
from jax import lax
from jax.sharding import PartitionSpec as P

NV = 16
NC = 32
PAIR_CHUNKS = 2


def swap(x, axis, bit):
    size = lax.axis_size(axis)
    return lax.ppermute(x, axis, [(i, i ^ bit) for i in range(size)])


def gather_axis(mine, axis):
    count = lax.axis_size(axis)
    me = lax.axis_index(axis)
    cur = mine[None]
    bit = count // 2
    while bit >= 1:
        got = swap(cur, axis, bit)
        low = (me & bit) == 0
        cur = jnp.where(low, jnp.stack([cur, got], 1), jnp.stack([got, cur], 1))
        cur = cur.reshape((-1,) + mine.shape)
        bit //= 2
    return cur


def scatter_sum_col(own_block, last_swap):
    col_count = lax.axis_size("col")
    acc = {}
    extra = None
    bit = 1
    while bit < col_count:
        deltas = [d for d in range(col_count) if d & bit and d % bit == 0]
        send = []
        for d in deltas:
            value = acc.pop(d) if d in acc else own_block(d)
            send.append(value)
        send = jnp.stack(send)
        if bit * 2 >= col_count:
            got, extra = last_swap(send, bit)
        else:
            got = swap(send, "col", bit)
        for i, d in enumerate(deltas):
            kept = d ^ bit
            base = acc.pop(kept) if kept in acc else own_block(kept)
            acc[kept] = base + got[i]
        bit *= 2
    return (acc[0] if 0 in acc else own_block(0)), extra


def screened_of(valence_a, valence_b, screening):
    col_count, chunk, _, mu_cols = valence_a.shape
    valence_a = valence_a.astype(jnp.float32)
    valence_b = valence_b.astype(jnp.float32)
    val_pairs = (valence_a[:, :, :, None, :] * valence_b[:, :, None, :, :]).astype(jnp.bfloat16)
    val_pairs = val_pairs.reshape(col_count, chunk * NV * NV, mu_cols)
    screen = screening.reshape(col_count, mu_cols, screening.shape[1])
    screened = lax.dot_general(
        val_pairs, screen, (((0, 2), (0, 1)), ((), ())), preferred_element_type=jnp.float32
    ).astype(jnp.bfloat16)
    return screened.reshape(chunk, NV * NV, screening.shape[1])


def body(orbitals, screening, pairs_k):
    k_dev, orb_count, mu_cols = orbitals.shape
    group_count = lax.axis_size("pb")
    col_count = lax.axis_size("col")
    kpoint_count = k_dev * group_count
    group_index = lax.axis_index("pb")
    col_index = lax.axis_index("col")
    kpoint_a = pairs_k[0]
    kpoint_b = (kpoint_a - group_index) % kpoint_count
    pair_count = kpoint_a.shape[0]

    wanted = jnp.concatenate([kpoint_a, kpoint_b])
    held_valence = gather_axis(orbitals[:, :NV, :], "pb").reshape(kpoint_count, NV, mu_cols)
    held_conduction = gather_axis(orbitals[:, NV:, :], "pb").reshape(
        kpoint_count, orb_count - NV, mu_cols
    )

    if kpoint_count <= wanted.shape[0]:
        valence = jnp.take(gather_axis(held_valence, "col"), wanted, axis=1, mode="clip")
    else:
        valence = gather_axis(jnp.take(held_valence, wanted, axis=0, mode="clip"), "col")
    conduction = jnp.take(held_conduction, wanted, axis=0, mode="clip").astype(jnp.float32)
    rows_per_block = NC // col_count
    chunk = pair_count // PAIR_CHUNKS
    starts = list(range(0, pair_count, chunk))

    def cond_block(first, delta):
        cond_a = conduction[first : first + chunk]
        cond_b = conduction[pair_count + first : pair_count + first + chunk]
        rows = lax.dynamic_slice_in_dim(
            cond_a, (col_index ^ delta) * rows_per_block, rows_per_block, 1
        )
        cond_pairs = (rows[:, :, None, :] * cond_b[:, None, :, :]).astype(jnp.bfloat16)
        return cond_pairs.reshape(chunk, rows_per_block * NC, mu_cols)

    cond_blocks = [[cond_block(first, d) for d in range(col_count)] for first in starts]
    valence, cond_blocks = lax.optimization_barrier((valence, cond_blocks))

    def valence_of(first):
        return (
            valence[:, first : first + chunk],
            valence[:, pair_count + first : pair_count + first + chunk],
        )

    results = []
    screened = screened_of(*valence_of(starts[0]), screening[0])
    for n_chunk, first in enumerate(starts):

        def own_block(delta, screened=screened, blocks=cond_blocks[n_chunk]):
            cond_pairs = blocks[delta]
            return jnp.einsum(
                "pan,pbn->pab", screened, cond_pairs, preferred_element_type=jnp.float32
            )

        def last_swap(send, bit):
            got = swap(send.astype(jnp.bfloat16), "col", bit)
            return got.astype(jnp.float32), None

        summed, _ = scatter_sum_col(own_block, last_swap)
        results.append(summed)
        if n_chunk + 1 < len(starts):
            screened = screened_of(*valence_of(starts[n_chunk + 1]), screening[0])
    return jnp.concatenate(results, 0)[None]


def solution(mesh):
    placed = (P("pb", None, "col"), P("pb", None, "col"), P("pb", None))
    return jax.shard_map(
        body, mesh=mesh, in_specs=placed, out_specs=P("pb", None, None, "col"), check_vma=False
    )
```

```python
import jax
import jax.numpy as jnp
from jax import lax
from jax.sharding import PartitionSpec as P

NV = 16
NC = 32
PAIR_CHUNKS = 2


def swap(x, axis, bit):
    size = lax.axis_size(axis)
    return lax.ppermute(x, axis, [(i, i ^ bit) for i in range(size)])


def gather_axis(mine, axis):
    count = lax.axis_size(axis)
    me = lax.axis_index(axis)
    cur = mine[None]
    bit = count // 2
    while bit >= 1:
        got = swap(cur, axis, bit)
        low = (me & bit) == 0
        cur = jnp.where(low, jnp.stack([cur, got], 1), jnp.stack([got, cur], 1))
        cur = cur.reshape((-1,) + mine.shape)
        bit //= 2
    return cur


def scatter_sum_col(own_block, last_swap):
    col_count = lax.axis_size("col")
    acc = {}
    extra = None
    bit = 1
    while bit < col_count:
        deltas = [d for d in range(col_count) if d & bit and d % bit == 0]
        send = []
        for d in deltas:
            value = acc.pop(d) if d in acc else own_block(d)
            send.append(value)
        send = jnp.stack(send)
        if bit * 2 >= col_count:
            got, extra = last_swap(send, bit)
        else:
            got = swap(send, "col", bit)
        for i, d in enumerate(deltas):
            kept = d ^ bit
            base = acc.pop(kept) if kept in acc else own_block(kept)
            acc[kept] = base + got[i]
        bit *= 2
    return (acc[0] if 0 in acc else own_block(0)), extra


def screened_of(valence_a, valence_b, screening):
    col_count, chunk, _, mu_cols = valence_a.shape
    valence_a = valence_a.astype(jnp.float32)
    valence_b = valence_b.astype(jnp.float32)
    val_pairs = (valence_a[:, :, :, None, :] * valence_b[:, :, None, :, :]).astype(jnp.bfloat16)
    val_pairs = val_pairs.reshape(col_count, chunk * NV * NV, mu_cols)
    screen = screening.reshape(col_count, mu_cols, screening.shape[1])
    screened = lax.dot_general(
        val_pairs, screen, (((0, 2), (0, 1)), ((), ())), preferred_element_type=jnp.float32
    ).astype(jnp.bfloat16)
    return screened.reshape(chunk, NV * NV, screening.shape[1])


def body(orbitals, screening, pairs_k):
    k_dev, orb_count, mu_cols = orbitals.shape
    group_count = lax.axis_size("pb")
    col_count = lax.axis_size("col")
    kpoint_count = k_dev * group_count
    group_index = lax.axis_index("pb")
    col_index = lax.axis_index("col")
    kpoint_a = pairs_k[0]
    kpoint_b = (kpoint_a - group_index) % kpoint_count
    pair_count = kpoint_a.shape[0]

    wanted = jnp.concatenate([kpoint_a, kpoint_b])
    held_valence = gather_axis(orbitals[:, :NV, :], "pb").reshape(kpoint_count, NV, mu_cols)
    held_conduction = gather_axis(orbitals[:, NV:, :], "pb").reshape(
        kpoint_count, orb_count - NV, mu_cols
    )

    valence = gather_axis(jnp.take(held_valence, wanted, axis=0, mode="clip"), "col")
    conduction = jnp.take(held_conduction, wanted, axis=0, mode="clip").astype(jnp.float32)
    rows_per_block = NC // col_count
    chunk = pair_count // PAIR_CHUNKS
    starts = list(range(0, pair_count, chunk))

    def cond_block(first, delta):
        cond_a = conduction[first : first + chunk]
        cond_b = conduction[pair_count + first : pair_count + first + chunk]
        rows = lax.dynamic_slice_in_dim(
            cond_a, (col_index ^ delta) * rows_per_block, rows_per_block, 1
        )
        cond_pairs = (rows[:, :, None, :] * cond_b[:, None, :, :]).astype(jnp.bfloat16)
        return cond_pairs.reshape(chunk, rows_per_block * NC, mu_cols)

    cond_blocks = [[cond_block(first, d) for d in range(col_count)] for first in starts]
    valence, cond_blocks = lax.optimization_barrier((valence, cond_blocks))

    def valence_of(first):
        return (
            valence[:, first : first + chunk],
            valence[:, pair_count + first : pair_count + first + chunk],
        )

    results = []
    screened = screened_of(*valence_of(starts[0]), screening[0])
    for n_chunk, first in enumerate(starts):

        def own_block(delta, screened=screened, blocks=cond_blocks[n_chunk]):
            cond_pairs = blocks[delta]
            return jnp.einsum(
                "pan,pbn->pab", screened, cond_pairs, preferred_element_type=jnp.float32
            )

        def last_swap(send, bit):
            got = swap(send.astype(jnp.bfloat16), "col", bit)
            return got.astype(jnp.float32), None

        summed, _ = scatter_sum_col(own_block, last_swap)
        results.append(summed)
        if n_chunk + 1 < len(starts):
            screened = screened_of(*valence_of(starts[n_chunk + 1]), screening[0])
    return jnp.concatenate(results, 0)[None]


def solution(mesh):
    placed = (P("pb", None, "col"), P("pb", None, "col"), P("pb", None))
    return jax.shard_map(
        body, mesh=mesh, in_specs=placed, out_specs=P("pb", None, None, "col"), check_vma=False
    )
```

```python
import jax
import jax.numpy as jnp
from jax import lax
from jax.sharding import PartitionSpec as P

NV = 16
NC = 32
PAIR_CHUNKS = 2


def gather_axis_xor(mine, axis):
    count = lax.axis_size(axis)
    cur = mine[None]
    bit = count // 2
    while bit >= 1:
        got = swap(cur, axis, bit)
        cur = jnp.stack([cur, got], 1).reshape((-1,) + mine.shape)
        bit //= 2
    return cur


def swap(x, axis, bit):
    size = lax.axis_size(axis)
    return lax.ppermute(x, axis, [(i, i ^ bit) for i in range(size)])


def gather_axis(mine, axis):
    count = lax.axis_size(axis)
    me = lax.axis_index(axis)
    cur = mine[None]
    bit = count // 2
    while bit >= 1:
        got = swap(cur, axis, bit)
        low = (me & bit) == 0
        cur = jnp.where(low, jnp.stack([cur, got], 1), jnp.stack([got, cur], 1))
        cur = cur.reshape((-1,) + mine.shape)
        bit //= 2
    return cur


def scatter_sum_col(own_block, last_swap):
    col_count = lax.axis_size("col")
    acc = {}
    extra = None
    bit = 1
    while bit < col_count:
        deltas = [d for d in range(col_count) if d & bit and d % bit == 0]
        send = []
        for d in deltas:
            value = acc.pop(d) if d in acc else own_block(d)
            send.append(value)
        send = jnp.stack(send)
        if bit * 2 >= col_count:
            got, extra = last_swap(send, bit)
        else:
            got = swap(send, "col", bit)
        for i, d in enumerate(deltas):
            kept = d ^ bit
            base = acc.pop(kept) if kept in acc else own_block(kept)
            acc[kept] = base + got[i]
        bit *= 2
    return (acc[0] if 0 in acc else own_block(0)), extra


def screened_of(valence_a, valence_b, screening):
    col_count, chunk, _, mu_cols = valence_a.shape
    valence_a = valence_a.astype(jnp.float32)
    valence_b = valence_b.astype(jnp.float32)
    val_pairs = (valence_a[:, :, :, None, :] * valence_b[:, :, None, :, :]).astype(jnp.bfloat16)
    val_pairs = val_pairs.reshape(col_count, chunk * NV * NV, mu_cols)
    screen = screening.reshape(col_count, mu_cols, screening.shape[1])
    screened = lax.dot_general(
        val_pairs, screen, (((0, 2), (0, 1)), ((), ())), preferred_element_type=jnp.float32
    ).astype(jnp.bfloat16)
    return screened.reshape(chunk, NV * NV, screening.shape[1])


def body(orbitals, screening, pairs_k):
    k_dev, orb_count, mu_cols = orbitals.shape
    group_count = lax.axis_size("pb")
    col_count = lax.axis_size("col")
    kpoint_count = k_dev * group_count
    group_index = lax.axis_index("pb")
    col_index = lax.axis_index("col")
    kpoint_a = pairs_k[0]
    kpoint_b = (kpoint_a - group_index) % kpoint_count
    pair_count = kpoint_a.shape[0]

    wanted = jnp.concatenate([kpoint_a, kpoint_b])
    wanted = ((wanted // k_dev) ^ group_index) * k_dev + wanted % k_dev
    held_valence = gather_axis_xor(orbitals[:, :NV, :], "pb").reshape(kpoint_count, NV, mu_cols)
    held_conduction = gather_axis_xor(orbitals[:, NV:, :], "pb").reshape(
        kpoint_count, orb_count - NV, mu_cols
    )

    valence = gather_axis(jnp.take(held_valence, wanted, axis=0, mode="clip"), "col")
    conduction = jnp.take(held_conduction, wanted, axis=0, mode="clip").astype(jnp.float32)
    rows_per_block = NC // col_count
    chunk = pair_count // PAIR_CHUNKS
    starts = list(range(0, pair_count, chunk))

    def cond_block(first, delta):
        cond_a = conduction[first : first + chunk]
        cond_b = conduction[pair_count + first : pair_count + first + chunk]
        rows = lax.dynamic_slice_in_dim(
            cond_a, (col_index ^ delta) * rows_per_block, rows_per_block, 1
        )
        cond_pairs = (rows[:, :, None, :] * cond_b[:, None, :, :]).astype(jnp.bfloat16)
        return cond_pairs.reshape(chunk, rows_per_block * NC, mu_cols)

    cond_blocks = [[cond_block(first, d) for d in range(col_count)] for first in starts]
    valence, cond_blocks = lax.optimization_barrier((valence, cond_blocks))

    def valence_of(first):
        return (
            valence[:, first : first + chunk],
            valence[:, pair_count + first : pair_count + first + chunk],
        )

    results = []
    screened = screened_of(*valence_of(starts[0]), screening[0])
    for n_chunk, first in enumerate(starts):

        def own_block(delta, screened=screened, blocks=cond_blocks[n_chunk]):
            cond_pairs = blocks[delta]
            return jnp.einsum(
                "pan,pbn->pab", screened, cond_pairs, preferred_element_type=jnp.float32
            )

        def last_swap(send, bit):
            got = swap(send.astype(jnp.bfloat16), "col", bit)
            return got.astype(jnp.float32), None

        summed, _ = scatter_sum_col(own_block, last_swap)
        results.append(summed)
        if n_chunk + 1 < len(starts):
            screened = screened_of(*valence_of(starts[n_chunk + 1]), screening[0])
    return jnp.concatenate(results, 0)[None]


def solution(mesh):
    placed = (P("pb", None, "col"), P("pb", None, "col"), P("pb", None))
    return jax.shard_map(
        body, mesh=mesh, in_specs=placed, out_specs=P("pb", None, None, "col"), check_vma=False
    )
```

```python
import jax
import jax.numpy as jnp
from jax import lax
from jax.sharding import PartitionSpec as P

NV = 16
NC = 32
PAIR_CHUNKS = 2


def swap(x, axis, bit):
    size = lax.axis_size(axis)
    return lax.ppermute(x, axis, [(i, i ^ bit) for i in range(size)])


def gather_axis(mine, axis):
    count = lax.axis_size(axis)
    me = lax.axis_index(axis)
    cur = mine[None]
    bit = count // 2
    while bit >= 1:
        got = swap(cur, axis, bit)
        low = (me & bit) == 0
        cur = jnp.where(low, jnp.stack([cur, got], 1), jnp.stack([got, cur], 1))
        cur = cur.reshape((-1,) + mine.shape)
        bit //= 2
    return cur


def scatter_sum_col(own_block, last_swap):
    col_count = lax.axis_size("col")
    acc = {}
    extra = None
    bit = 1
    while bit < col_count:
        deltas = [d for d in range(col_count) if d & bit and d % bit == 0]
        send = []
        for d in deltas:
            value = acc.pop(d) if d in acc else own_block(d)
            send.append(value)
        send = jnp.stack(send)
        if bit * 2 >= col_count:
            got, extra = last_swap(send, bit)
        else:
            got = swap(send, "col", bit)
        for i, d in enumerate(deltas):
            kept = d ^ bit
            base = acc.pop(kept) if kept in acc else own_block(kept)
            acc[kept] = base + got[i]
        bit *= 2
    return (acc[0] if 0 in acc else own_block(0)), extra


def screened_of(valence_a, valence_b, screening):
    col_count, chunk, _, mu_cols = valence_a.shape
    val_pairs = valence_a[:, :, :, None, :] * valence_b[:, :, None, :, :]
    val_pairs = val_pairs.reshape(col_count, chunk * NV * NV, mu_cols)
    screen = screening.reshape(col_count, mu_cols, screening.shape[1])
    screened = lax.dot_general(
        val_pairs, screen, (((0, 2), (0, 1)), ((), ())), preferred_element_type=jnp.float32
    ).astype(jnp.bfloat16)
    return screened.reshape(chunk, NV * NV, screening.shape[1])


def body(orbitals, screening, pairs_k):
    k_dev, orb_count, mu_cols = orbitals.shape
    group_count = lax.axis_size("pb")
    col_count = lax.axis_size("col")
    kpoint_count = k_dev * group_count
    group_index = lax.axis_index("pb")
    col_index = lax.axis_index("col")
    kpoint_a = pairs_k[0]
    kpoint_b = (kpoint_a - group_index) % kpoint_count
    pair_count = kpoint_a.shape[0]

    wanted = jnp.concatenate([kpoint_a, kpoint_b])
    held_valence = gather_axis(orbitals[:, :NV, :], "pb").reshape(kpoint_count, NV, mu_cols)
    held_conduction = gather_axis(orbitals[:, NV:, :], "pb").reshape(
        kpoint_count, orb_count - NV, mu_cols
    )

    valence = gather_axis(jnp.take(held_valence, wanted, axis=0, mode="clip"), "col")
    conduction = jnp.take(held_conduction, wanted, axis=0, mode="clip").astype(jnp.float32)
    rows_per_block = NC // col_count
    chunk = pair_count // PAIR_CHUNKS
    starts = list(range(0, pair_count, chunk))

    def cond_block(first, delta):
        cond_a = conduction[first : first + chunk]
        cond_b = conduction[pair_count + first : pair_count + first + chunk]
        rows = lax.dynamic_slice_in_dim(
            cond_a, (col_index ^ delta) * rows_per_block, rows_per_block, 1
        )
        cond_pairs = (rows[:, :, None, :] * cond_b[:, None, :, :]).astype(jnp.bfloat16)
        return cond_pairs.reshape(chunk, rows_per_block * NC, mu_cols)

    cond_blocks = [[cond_block(first, d) for d in range(col_count)] for first in starts]
    valence, cond_blocks = lax.optimization_barrier((valence, cond_blocks))

    def valence_of(first):
        return (
            valence[:, first : first + chunk],
            valence[:, pair_count + first : pair_count + first + chunk],
        )

    results = []
    screened = screened_of(*valence_of(starts[0]), screening[0])
    for n_chunk, first in enumerate(starts):

        def own_block(delta, screened=screened, blocks=cond_blocks[n_chunk]):
            cond_pairs = blocks[delta]
            return jnp.einsum(
                "pan,pbn->pab", screened, cond_pairs, preferred_element_type=jnp.float32
            )

        def last_swap(send, bit):
            got = swap(send.astype(jnp.bfloat16), "col", bit)
            return got.astype(jnp.float32), None

        summed, _ = scatter_sum_col(own_block, last_swap)
        results.append(summed)
        if n_chunk + 1 < len(starts):
            screened = screened_of(*valence_of(starts[n_chunk + 1]), screening[0])
    return jnp.concatenate(results, 0)[None]


def solution(mesh):
    placed = (P("pb", None, "col"), P("pb", None, "col"), P("pb", None))
    return jax.shard_map(
        body, mesh=mesh, in_specs=placed, out_specs=P("pb", None, None, "col"), check_vma=False
    )
```

```python
import jax
import jax.numpy as jnp
from jax import lax
from jax.sharding import PartitionSpec as P

NV = 16
NC = 32
PAIR_CHUNKS = 2


def swap(x, axis, bit):
    size = lax.axis_size(axis)
    return lax.ppermute(x, axis, [(i, i ^ bit) for i in range(size)])


def gather_axis(mine, axis):
    count = lax.axis_size(axis)
    me = lax.axis_index(axis)
    cur = mine[None]
    bit = count // 2
    while bit >= 1:
        got = swap(cur, axis, bit)
        low = (me & bit) == 0
        cur = jnp.where(low, jnp.stack([cur, got], 1), jnp.stack([got, cur], 1))
        cur = cur.reshape((-1,) + mine.shape)
        bit //= 2
    return cur


def scatter_sum_col(own_block, last_swap):
    col_count = lax.axis_size("col")
    acc = {}
    extra = None
    bit = 1
    while bit < col_count:
        deltas = [d for d in range(col_count) if d & bit and d % bit == 0]
        send = []
        for d in deltas:
            value = acc.pop(d) if d in acc else own_block(d)
            send.append(value)
        send = jnp.stack(send)
        if bit * 2 >= col_count:
            got, extra = last_swap(send, bit)
        else:
            got = swap(send, "col", bit)
        for i, d in enumerate(deltas):
            kept = d ^ bit
            base = acc.pop(kept) if kept in acc else own_block(kept)
            acc[kept] = base + got[i]
        bit *= 2
    return (acc[0] if 0 in acc else own_block(0)), extra


def screened_of(valence_a, valence_b, screening):
    col_count, chunk, _, mu_cols = valence_a.shape
    val_pairs = valence_a[:, :, :, None, :] * valence_b[:, :, None, :, :]
    val_pairs = val_pairs.reshape(col_count, chunk * NV * NV, mu_cols)
    screen = screening.reshape(col_count, mu_cols, screening.shape[1])
    screened = lax.dot_general(
        val_pairs, screen, (((0, 2), (0, 1)), ((), ())), preferred_element_type=jnp.float32
    ).astype(jnp.bfloat16)
    return screened.reshape(chunk, NV * NV, screening.shape[1])


def body(orbitals, screening, pairs_k):
    k_dev, orb_count, mu_cols = orbitals.shape
    group_count = lax.axis_size("pb")
    col_count = lax.axis_size("col")
    kpoint_count = k_dev * group_count
    group_index = lax.axis_index("pb")
    col_index = lax.axis_index("col")
    kpoint_a = pairs_k[0]
    kpoint_b = (kpoint_a - group_index) % kpoint_count
    pair_count = kpoint_a.shape[0]

    wanted = jnp.concatenate([kpoint_a, kpoint_b])
    held_valence = gather_axis(orbitals[:, :NV, :], "pb").reshape(kpoint_count, NV, mu_cols)
    held_conduction = gather_axis(orbitals[:, NV:, :], "pb").reshape(
        kpoint_count, orb_count - NV, mu_cols
    )

    valence = gather_axis(jnp.take(held_valence, wanted, axis=0, mode="clip"), "col")
    conduction = jnp.take(held_conduction, wanted, axis=0, mode="clip")
    rows_per_block = NC // col_count
    chunk = pair_count // PAIR_CHUNKS
    starts = list(range(0, pair_count, chunk))

    def cond_block(first, delta):
        cond_a = conduction[first : first + chunk]
        cond_b = conduction[pair_count + first : pair_count + first + chunk]
        rows = lax.dynamic_slice_in_dim(
            cond_a, (col_index ^ delta) * rows_per_block, rows_per_block, 1
        )
        cond_pairs = rows[:, :, None, :] * cond_b[:, None, :, :]
        return cond_pairs.reshape(chunk, rows_per_block * NC, mu_cols)

    cond_blocks = [[cond_block(first, d) for d in range(col_count)] for first in starts]
    valence, cond_blocks = lax.optimization_barrier((valence, cond_blocks))

    def valence_of(first):
        return (
            valence[:, first : first + chunk],
            valence[:, pair_count + first : pair_count + first + chunk],
        )

    results = []
    screened = screened_of(*valence_of(starts[0]), screening[0])
    for n_chunk, first in enumerate(starts):

        def own_block(delta, screened=screened, blocks=cond_blocks[n_chunk]):
            cond_pairs = blocks[delta]
            return jnp.einsum(
                "pan,pbn->pab", screened, cond_pairs, preferred_element_type=jnp.float32
            )

        def last_swap(send, bit):
            got = swap(send.astype(jnp.bfloat16), "col", bit)
            return got.astype(jnp.float32), None

        summed, _ = scatter_sum_col(own_block, last_swap)
        results.append(summed)
        if n_chunk + 1 < len(starts):
            screened = screened_of(*valence_of(starts[n_chunk + 1]), screening[0])
    return jnp.concatenate(results, 0)[None]


def solution(mesh):
    placed = (P("pb", None, "col"), P("pb", None, "col"), P("pb", None))
    return jax.shard_map(
        body, mesh=mesh, in_specs=placed, out_specs=P("pb", None, None, "col"), check_vma=False
    )
```

```python
import jax
import jax.numpy as jnp
from jax import lax
from jax.sharding import PartitionSpec as P

NV = 16
NC = 32
PAIR_CHUNKS = 1


def swap(x, axis, bit):
    size = lax.axis_size(axis)
    return lax.ppermute(x, axis, [(i, i ^ bit) for i in range(size)])


def gather_axis(mine, axis):
    count = lax.axis_size(axis)
    me = lax.axis_index(axis)
    cur = mine[None]
    bit = count // 2
    while bit >= 1:
        got = swap(cur, axis, bit)
        low = (me & bit) == 0
        cur = jnp.where(low, jnp.stack([cur, got], 1), jnp.stack([got, cur], 1))
        cur = cur.reshape((-1,) + mine.shape)
        bit //= 2
    return cur


def scatter_sum_col(own_block, last_swap):
    col_count = lax.axis_size("col")
    acc = {}
    extra = None
    bit = 1
    while bit < col_count:
        deltas = [d for d in range(col_count) if d & bit and d % bit == 0]
        send = []
        for d in deltas:
            value = acc.pop(d) if d in acc else own_block(d)
            send.append(value)
        send = jnp.stack(send)
        if bit * 2 >= col_count:
            got, extra = last_swap(send, bit)
        else:
            got = swap(send, "col", bit)
        for i, d in enumerate(deltas):
            kept = d ^ bit
            base = acc.pop(kept) if kept in acc else own_block(kept)
            acc[kept] = base + got[i]
        bit *= 2
    return (acc[0] if 0 in acc else own_block(0)), extra


def screened_of(valence_a, valence_b, screening):
    col_count, chunk, _, mu_cols = valence_a.shape
    val_pairs = valence_a[:, :, :, None, :] * valence_b[:, :, None, :, :]
    val_pairs = val_pairs.reshape(col_count, chunk * NV * NV, mu_cols)
    screen = screening.reshape(col_count, mu_cols, screening.shape[1])
    screened = lax.dot_general(
        val_pairs, screen, (((0, 2), (0, 1)), ((), ())), preferred_element_type=jnp.float32
    ).astype(jnp.bfloat16)
    return screened.reshape(chunk, NV * NV, screening.shape[1])


def body(orbitals, screening, pairs_k):
    k_dev, orb_count, mu_cols = orbitals.shape
    group_count = lax.axis_size("pb")
    col_count = lax.axis_size("col")
    kpoint_count = k_dev * group_count
    group_index = lax.axis_index("pb")
    col_index = lax.axis_index("col")
    kpoint_a = pairs_k[0]
    kpoint_b = (kpoint_a - group_index) % kpoint_count
    pair_count = kpoint_a.shape[0]

    wanted = jnp.concatenate([kpoint_a, kpoint_b])
    held_valence = gather_axis(orbitals[:, :NV, :], "pb").reshape(kpoint_count, NV, mu_cols)
    held_conduction = gather_axis(orbitals[:, NV:, :], "pb").reshape(
        kpoint_count, orb_count - NV, mu_cols
    )

    valence = gather_axis(jnp.take(held_valence, wanted, axis=0, mode="clip"), "col")
    conduction = jnp.take(held_conduction, wanted, axis=0, mode="clip")
    rows_per_block = NC // col_count
    chunk = pair_count // PAIR_CHUNKS
    starts = list(range(0, pair_count, chunk))

    def cond_block(first, delta):
        cond_a = conduction[first : first + chunk]
        cond_b = conduction[pair_count + first : pair_count + first + chunk]
        rows = lax.dynamic_slice_in_dim(
            cond_a, (col_index ^ delta) * rows_per_block, rows_per_block, 1
        )
        cond_pairs = rows[:, :, None, :] * cond_b[:, None, :, :]
        return cond_pairs.reshape(chunk, rows_per_block * NC, mu_cols)

    cond_blocks = [[cond_block(first, d) for d in range(col_count)] for first in starts]
    valence, cond_blocks = lax.optimization_barrier((valence, cond_blocks))

    def valence_of(first):
        return (
            valence[:, first : first + chunk],
            valence[:, pair_count + first : pair_count + first + chunk],
        )

    results = []
    screened = screened_of(*valence_of(starts[0]), screening[0])
    for n_chunk, first in enumerate(starts):

        def own_block(delta, screened=screened, blocks=cond_blocks[n_chunk]):
            cond_pairs = blocks[delta]
            return jnp.einsum(
                "pan,pbn->pab", screened, cond_pairs, preferred_element_type=jnp.float32
            )

        def last_swap(send, bit):
            got = swap(send.astype(jnp.bfloat16), "col", bit)
            return got.astype(jnp.float32), None

        summed, _ = scatter_sum_col(own_block, last_swap)
        results.append(summed)
        if n_chunk + 1 < len(starts):
            screened = screened_of(*valence_of(starts[n_chunk + 1]), screening[0])
    return jnp.concatenate(results, 0)[None]


def solution(mesh):
    placed = (P("pb", None, "col"), P("pb", None, "col"), P("pb", None))
    return jax.shard_map(
        body, mesh=mesh, in_specs=placed, out_specs=P("pb", None, None, "col"), check_vma=False
    )
```

```python
import jax
import jax.numpy as jnp
from jax import lax
from jax.sharding import PartitionSpec as P

NV = 16
NC = 32
PAIR_CHUNKS = 2


def gather_axis_xor(mine, axis):
    count = lax.axis_size(axis)
    cur = mine[None]
    bit = count // 2
    while bit >= 1:
        got = swap(cur, axis, bit)
        cur = jnp.stack([cur, got], 1).reshape((-1,) + mine.shape)
        bit //= 2
    return cur


def swap(x, axis, bit):
    size = lax.axis_size(axis)
    return lax.ppermute(x, axis, [(i, i ^ bit) for i in range(size)])


def gather_axis(mine, axis):
    count = lax.axis_size(axis)
    me = lax.axis_index(axis)
    cur = mine[None]
    bit = count // 2
    while bit >= 1:
        got = swap(cur, axis, bit)
        low = (me & bit) == 0
        cur = jnp.where(low, jnp.stack([cur, got], 1), jnp.stack([got, cur], 1))
        cur = cur.reshape((-1,) + mine.shape)
        bit //= 2
    return cur


def scatter_sum_col(own_block, last_swap):
    col_count = lax.axis_size("col")
    acc = {}
    extra = None
    bit = 1
    while bit < col_count:
        deltas = [d for d in range(col_count) if d & bit and d % bit == 0]
        send = []
        for d in deltas:
            value = acc.pop(d) if d in acc else own_block(d)
            send.append(value)
        send = jnp.stack(send)
        if bit * 2 >= col_count:
            got, extra = last_swap(send, bit)
        else:
            got = swap(send, "col", bit)
        for i, d in enumerate(deltas):
            kept = d ^ bit
            base = acc.pop(kept) if kept in acc else own_block(kept)
            acc[kept] = base + got[i]
        bit *= 2
    return (acc[0] if 0 in acc else own_block(0)), extra


def screened_of(valence_a, valence_b, screening):
    col_count, chunk, _, mu_cols = valence_a.shape
    val_pairs = valence_a[:, :, :, None, :] * valence_b[:, :, None, :, :]
    val_pairs = val_pairs.reshape(col_count, chunk * NV * NV, mu_cols)
    screen = screening.reshape(col_count, mu_cols, screening.shape[1])
    screened = lax.dot_general(
        val_pairs, screen, (((0, 2), (0, 1)), ((), ())), preferred_element_type=jnp.float32
    ).astype(jnp.bfloat16)
    return screened.reshape(chunk, NV * NV, screening.shape[1])


def body(orbitals, screening, pairs_k):
    k_dev, orb_count, mu_cols = orbitals.shape
    group_count = lax.axis_size("pb")
    col_count = lax.axis_size("col")
    kpoint_count = k_dev * group_count
    group_index = lax.axis_index("pb")
    col_index = lax.axis_index("col")
    kpoint_a = pairs_k[0]
    kpoint_b = (kpoint_a - group_index) % kpoint_count
    pair_count = kpoint_a.shape[0]

    wanted = jnp.concatenate([kpoint_a, kpoint_b])
    wanted = ((wanted // k_dev) ^ group_index) * k_dev + wanted % k_dev
    held_valence = gather_axis_xor(orbitals[:, :NV, :], "pb").reshape(kpoint_count, NV, mu_cols)
    held_conduction = gather_axis_xor(orbitals[:, NV:, :], "pb").reshape(
        kpoint_count, orb_count - NV, mu_cols
    )

    valence = gather_axis(jnp.take(held_valence, wanted, axis=0, mode="clip"), "col")
    conduction = jnp.take(held_conduction, wanted, axis=0, mode="clip")
    rows_per_block = NC // col_count
    chunk = pair_count // PAIR_CHUNKS
    starts = list(range(0, pair_count, chunk))

    def cond_block(first, delta):
        cond_a = conduction[first : first + chunk]
        cond_b = conduction[pair_count + first : pair_count + first + chunk]
        rows = lax.dynamic_slice_in_dim(
            cond_a, (col_index ^ delta) * rows_per_block, rows_per_block, 1
        )
        cond_pairs = rows[:, :, None, :] * cond_b[:, None, :, :]
        return cond_pairs.reshape(chunk, rows_per_block * NC, mu_cols)

    cond_blocks = [[cond_block(first, d) for d in range(col_count)] for first in starts]
    valence, cond_blocks = lax.optimization_barrier((valence, cond_blocks))

    def valence_of(first):
        return (
            valence[:, first : first + chunk],
            valence[:, pair_count + first : pair_count + first + chunk],
        )

    results = []
    screened = screened_of(*valence_of(starts[0]), screening[0])
    for n_chunk, first in enumerate(starts):

        def own_block(delta, screened=screened, blocks=cond_blocks[n_chunk]):
            cond_pairs = blocks[delta]
            return jnp.einsum(
                "pan,pbn->pab", screened, cond_pairs, preferred_element_type=jnp.float32
            )

        def last_swap(send, bit):
            got = swap(send.astype(jnp.bfloat16), "col", bit)
            return got.astype(jnp.float32), None

        summed, _ = scatter_sum_col(own_block, last_swap)
        results.append(summed)
        if n_chunk + 1 < len(starts):
            screened = screened_of(*valence_of(starts[n_chunk + 1]), screening[0])
    return jnp.concatenate(results, 0)[None]


def solution(mesh):
    placed = (P("pb", None, "col"), P("pb", None, "col"), P("pb", None))
    return jax.shard_map(
        body, mesh=mesh, in_specs=placed, out_specs=P("pb", None, None, "col"), check_vma=False
    )
```

```python
import jax
import jax.numpy as jnp
from jax import lax
from jax.sharding import PartitionSpec as P

NV = 16
NC = 32
PAIR_CHUNKS = 4


def swap(x, axis, bit):
    size = lax.axis_size(axis)
    return lax.ppermute(x, axis, [(i, i ^ bit) for i in range(size)])


def gather_axis(mine, axis):
    count = lax.axis_size(axis)
    me = lax.axis_index(axis)
    cur = mine[None]
    bit = count // 2
    while bit >= 1:
        got = swap(cur, axis, bit)
        low = (me & bit) == 0
        cur = jnp.where(low, jnp.stack([cur, got], 1), jnp.stack([got, cur], 1))
        cur = cur.reshape((-1,) + mine.shape)
        bit //= 2
    return cur


def scatter_sum_col(own_block, last_swap):
    col_count = lax.axis_size("col")
    acc = {}
    extra = None
    bit = 1
    while bit < col_count:
        deltas = [d for d in range(col_count) if d & bit and d % bit == 0]
        send = []
        for d in deltas:
            value = acc.pop(d) if d in acc else own_block(d)
            send.append(value)
        send = jnp.stack(send)
        if bit * 2 >= col_count:
            got, extra = last_swap(send, bit)
        else:
            got = swap(send, "col", bit)
        for i, d in enumerate(deltas):
            kept = d ^ bit
            base = acc.pop(kept) if kept in acc else own_block(kept)
            acc[kept] = base + got[i]
        bit *= 2
    return (acc[0] if 0 in acc else own_block(0)), extra


def screened_of(valence_a, valence_b, screening):
    col_count, chunk, _, mu_cols = valence_a.shape
    val_pairs = valence_a[:, :, :, None, :] * valence_b[:, :, None, :, :]
    val_pairs = val_pairs.reshape(col_count, chunk * NV * NV, mu_cols)
    screen = screening.reshape(col_count, mu_cols, screening.shape[1])
    screened = lax.dot_general(
        val_pairs, screen, (((0, 2), (0, 1)), ((), ())), preferred_element_type=jnp.float32
    ).astype(jnp.bfloat16)
    return screened.reshape(chunk, NV * NV, screening.shape[1])


def body(orbitals, screening, pairs_k):
    k_dev, orb_count, mu_cols = orbitals.shape
    group_count = lax.axis_size("pb")
    col_count = lax.axis_size("col")
    kpoint_count = k_dev * group_count
    group_index = lax.axis_index("pb")
    col_index = lax.axis_index("col")
    kpoint_a = pairs_k[0]
    kpoint_b = (kpoint_a - group_index) % kpoint_count
    pair_count = kpoint_a.shape[0]

    wanted = jnp.concatenate([kpoint_a, kpoint_b])
    held_valence = gather_axis(orbitals[:, :NV, :], "pb").reshape(kpoint_count, NV, mu_cols)
    held_conduction = gather_axis(orbitals[:, NV:, :], "pb").reshape(
        kpoint_count, orb_count - NV, mu_cols
    )

    valence = gather_axis(jnp.take(held_valence, wanted, axis=0, mode="clip"), "col")
    conduction = jnp.take(held_conduction, wanted, axis=0, mode="clip")
    rows_per_block = NC // col_count
    chunk = pair_count // PAIR_CHUNKS
    starts = list(range(0, pair_count, chunk))

    def cond_block(first, delta):
        cond_a = conduction[first : first + chunk]
        cond_b = conduction[pair_count + first : pair_count + first + chunk]
        rows = lax.dynamic_slice_in_dim(
            cond_a, (col_index ^ delta) * rows_per_block, rows_per_block, 1
        )
        cond_pairs = rows[:, :, None, :] * cond_b[:, None, :, :]
        return cond_pairs.reshape(chunk, rows_per_block * NC, mu_cols)

    cond_blocks = [[cond_block(first, d) for d in range(col_count)] for first in starts]
    valence, cond_blocks = lax.optimization_barrier((valence, cond_blocks))

    def valence_of(first):
        return (
            valence[:, first : first + chunk],
            valence[:, pair_count + first : pair_count + first + chunk],
        )

    results = []
    screened = screened_of(*valence_of(starts[0]), screening[0])
    for n_chunk, first in enumerate(starts):

        def own_block(delta, screened=screened, blocks=cond_blocks[n_chunk]):
            cond_pairs = blocks[delta]
            return jnp.einsum(
                "pan,pbn->pab", screened, cond_pairs, preferred_element_type=jnp.float32
            )

        def last_swap(send, bit):
            got = swap(send.astype(jnp.bfloat16), "col", bit)
            return got.astype(jnp.float32), None

        summed, _ = scatter_sum_col(own_block, last_swap)
        results.append(summed)
        if n_chunk + 1 < len(starts):
            screened = screened_of(*valence_of(starts[n_chunk + 1]), screening[0])
    return jnp.concatenate(results, 0)[None]


def solution(mesh):
    placed = (P("pb", None, "col"), P("pb", None, "col"), P("pb", None))
    return jax.shard_map(
        body, mesh=mesh, in_specs=placed, out_specs=P("pb", None, None, "col"), check_vma=False
    )
```

```python
import jax
import jax.numpy as jnp
from jax import lax
from jax.sharding import PartitionSpec as P

NV = 16
NC = 32
PAIR_CHUNKS = 2


def swap(x, axis, bit):
    size = lax.axis_size(axis)
    return lax.ppermute(x, axis, [(i, i ^ bit) for i in range(size)])


def gather_axis(mine, axis):
    count = lax.axis_size(axis)
    me = lax.axis_index(axis)
    cur = mine[None]
    bit = count // 2
    while bit >= 1:
        got = swap(cur, axis, bit)
        low = (me & bit) == 0
        cur = jnp.where(low, jnp.stack([cur, got], 1), jnp.stack([got, cur], 1))
        cur = cur.reshape((-1,) + mine.shape)
        bit //= 2
    return cur


def scatter_sum_col(own_block, last_swap):
    col_count = lax.axis_size("col")
    acc = {}
    extra = None
    bit = 1
    while bit < col_count:
        deltas = [d for d in range(col_count) if d & bit and d % bit == 0]
        send = []
        for d in deltas:
            value = acc.pop(d) if d in acc else own_block(d)
            send.append(value)
        send = jnp.stack(send)
        if bit * 2 >= col_count:
            got, extra = last_swap(send, bit)
        else:
            got = swap(send, "col", bit)
        for i, d in enumerate(deltas):
            kept = d ^ bit
            base = acc.pop(kept) if kept in acc else own_block(kept)
            acc[kept] = base + got[i]
        bit *= 2
    return (acc[0] if 0 in acc else own_block(0)), extra


def screened_of(valence_a, valence_b, screening):
    col_count, chunk, _, mu_cols = valence_a.shape
    val_pairs = valence_a[:, :, :, None, :] * valence_b[:, :, None, :, :]
    val_pairs = val_pairs.reshape(col_count, chunk * NV * NV, mu_cols)
    screen = screening.reshape(col_count, mu_cols, screening.shape[1])
    screened = lax.dot_general(
        val_pairs, screen, (((0, 2), (0, 1)), ((), ())), preferred_element_type=jnp.float32
    ).astype(jnp.bfloat16)
    return screened.reshape(chunk, NV * NV, screening.shape[1])


def body(orbitals, screening, pairs_k):
    k_dev, orb_count, mu_cols = orbitals.shape
    group_count = lax.axis_size("pb")
    col_count = lax.axis_size("col")
    kpoint_count = k_dev * group_count
    group_index = lax.axis_index("pb")
    col_index = lax.axis_index("col")
    kpoint_a = pairs_k[0]
    kpoint_b = (kpoint_a - group_index) % kpoint_count
    pair_count = kpoint_a.shape[0]

    wanted = jnp.concatenate([kpoint_a, kpoint_b])
    held_valence = gather_axis(orbitals[:, :NV, :], "pb").reshape(kpoint_count, NV, mu_cols)
    held_conduction = gather_axis(orbitals[:, NV:, :], "pb").reshape(
        kpoint_count, orb_count - NV, mu_cols
    )

    valence = gather_axis(jnp.take(held_valence, wanted, axis=0, mode="clip"), "col")
    conduction = jnp.take(held_conduction, wanted, axis=0, mode="clip")
    rows_per_block = NC // col_count
    chunk = pair_count // PAIR_CHUNKS
    starts = list(range(0, pair_count, chunk))

    def cond_block(first, delta):
        cond_a = conduction[first : first + chunk]
        cond_b = conduction[pair_count + first : pair_count + first + chunk]
        rows = lax.dynamic_slice_in_dim(
            cond_a.astype(jnp.float32), (col_index ^ delta) * rows_per_block, rows_per_block, 1
        ).astype(jnp.bfloat16)
        cond_pairs = rows[:, :, None, :] * cond_b[:, None, :, :]
        return cond_pairs.reshape(chunk, rows_per_block * NC, mu_cols)

    cond_blocks = [[cond_block(first, d) for d in range(col_count)] for first in starts]
    valence, cond_blocks = lax.optimization_barrier((valence, cond_blocks))

    def valence_of(first):
        return (
            valence[:, first : first + chunk],
            valence[:, pair_count + first : pair_count + first + chunk],
        )

    results = []
    screened = screened_of(*valence_of(starts[0]), screening[0])
    for n_chunk, first in enumerate(starts):

        def own_block(delta, screened=screened, blocks=cond_blocks[n_chunk]):
            cond_pairs = blocks[delta]
            return jnp.einsum(
                "pan,pbn->pab", screened, cond_pairs, preferred_element_type=jnp.float32
            )

        def last_swap(send, bit):
            got = swap(send.astype(jnp.bfloat16), "col", bit)
            return got.astype(jnp.float32), None

        summed, _ = scatter_sum_col(own_block, last_swap)
        results.append(summed)
        if n_chunk + 1 < len(starts):
            screened = screened_of(*valence_of(starts[n_chunk + 1]), screening[0])
    return jnp.concatenate(results, 0)[None]


def solution(mesh):
    placed = (P("pb", None, "col"), P("pb", None, "col"), P("pb", None))
    return jax.shard_map(
        body, mesh=mesh, in_specs=placed, out_specs=P("pb", None, None, "col"), check_vma=False
    )
```
